32 devices in a mesh: prow: 4 (over x, core), pcol: 8 (over z, y).
Axes of the slice: x: 2, y: 2, z: 4, core: 2. Of those that a mesh axis runs over, the one named last changes fastest.
Arguments:
- features: bfloat16 [8192, 512], P(('prow', 'pcol')), may hold values from -6 to 6
- tile_values: bfloat16 [4, 8, 128, 128, 128], P('prow', 'pcol'), may hold values from 0.0009994507 to 1
- tile_rows: int32 [4, 8, 128], P('prow', 'pcol'), may hold values from 0 to 15, as said below
- tile_cols: int32 [4, 8, 128], P('prow', 'pcol'), may hold values from 0 to 7, as said below
- tile_count: int32 [4, 8], P('prow', 'pcol'), may hold values from 32 to 128, as said below
- hub_local: int32 [4, 8, 8], P('prow', 'pcol'), may hold values from 0 to 255, as said below
- hub_edges: bfloat16 [8192, 256], P(('prow', 'pcol')), may hold values from 0.5 to 2
- w_self: bfloat16 [512, 512], replicated, may hold values from -0.25 to 0.25
- w_neigh: bfloat16 [512, 512], replicated, may hold values from -12 to 12
- bias: float32 [512], replicated, may hold values from -3 to 3
- cotangent: bfloat16 [8192, 512], P(('prow', 'pcol')), may hold values from -6 to 6
Outputs:
- activations: bfloat16 [8192, 512], P(('prow', 'pcol'))
- grad_features: bfloat16 [8192, 512], P(('prow', 'pcol'))
- grad_w_self: float32 [512, 512], replicated
- grad_w_neigh: float32 [512, 512], replicated
- grad_bias: float32 [512], replicated
The draws below stay inside these ranges and needn't reach their ends.
Inputs may be any that keep to these rules, and one draw needn't show every extreme that they name: On partition (i, j) the live slots (s < tile_count[i, j]) name distinct (tile_rows, tile_cols) pairs; slots 0 and 1 are always live. `tile_cols`: see tile_rows. `tile_count`: each partition's count is 128, 64 or 32. `hub_local`: distinct on each device.
All inputs are finite; a program needn't handle non-finite values.
Results may differ from the reference program's by a relative error of at most 0.008.
Values may be sent and summed in bfloat16 or wider, within the bound.
No kernel may reach another device: no remote copies, remote signals or barrier semaphores. Data moves between devices by JAX's collectives and lax.ppermute only.
A program may use at most 128 MiB of HBM per device.

```python
import math
import jax
import jax.numpy as jnp
from jax import lax

F = 512
TILE = 128
V_DEV = 256
HUB_DEV = 8
TILES = 128
HUBS = 256
VERTS = 8192
N_PROW = 4
N_PCOL = 8


def force_ends(order, top):
    first = jnp.argmax(order == top - 1)
    order = order.at[first].set(order[0]).at[0].set(top - 1)
    second = jnp.argmax(order == 0)
    order = order.at[second].set(order[1]).at[1].set(0)
    return order


def force_first(order, value):
    where_now = jnp.argmax(order == value)
    return order.at[where_now].set(order[0]).at[0].set(value)


def tile_pattern(key):
    part_count = N_PROW * N_PCOL
    row_tiles = N_PCOL * V_DEV // TILE
    col_tiles = N_PROW * V_DEV // TILE
    positions = row_tiles * col_tiles
    key_perm, key_shift, key_busy = jax.random.split(jax.random.fold_in(key, 11), 3)
    part_keys = jax.random.split(key_perm, part_count)

    def one_part(part_key):
        order = jax.random.permutation(part_key, positions).astype(jnp.int32)
        return force_ends(order, positions)[:TILES]
    chosen = jax.vmap(one_part)(part_keys)
    row_ids = (chosen // col_tiles).astype(jnp.int32).reshape(N_PROW, N_PCOL, TILES)
    col_ids = (chosen % col_tiles).astype(jnp.int32).reshape(N_PROW, N_PCOL, TILES)
    shifts = jax.random.randint(key_shift, (part_count,), 0, 3).astype(jnp.int32)
    counts = (TILES // jnp.left_shift(jnp.int32(1), shifts)).astype(jnp.int32)
    busiest = jax.random.randint(key_busy, (), 0, part_count).astype(jnp.int32)
    part_ids = jnp.arange(part_count, dtype=jnp.int32)
    counts = jnp.where(part_ids == busiest, jnp.int32(TILES), counts)
    counts = jnp.where(part_ids == (busiest + 1) % part_count, jnp.int32(TILES // 4), counts)
    return (row_ids, col_ids, counts.reshape(N_PROW, N_PCOL).astype(jnp.int32))


def draw_tile_rows(key, part):
    return tile_pattern(key)[0]


def draw_tile_cols(key, part):
    return tile_pattern(key)[1]


def draw_tile_count(key, part):
    return tile_pattern(key)[2]


def draw_hub_local(key, part):
    part_count = N_PROW * N_PCOL
    part_keys = jax.random.split(jax.random.fold_in(key, 23), part_count)
    part_ids = jnp.arange(part_count, dtype=jnp.int32)

    def one_part(part_key, part_id):
        order = jax.random.permutation(part_key, V_DEV).astype(jnp.int32)
        with_top = force_first(order, jnp.int32(V_DEV - 1))
        with_zero = force_first(order, jnp.int32(0))
        order = jnp.where(part_id == 0, with_top, jnp.where(part_id == 1, with_zero, order))
        return order[:HUB_DEV]
    return jax.vmap(one_part)(part_keys, part_ids).reshape(N_PROW, N_PCOL, HUB_DEV).astype(jnp.int32)


def levels(own_key, dims, cuts, low, top_value):
    def one(dim, shards_of):
        heights = jax.random.uniform(jax.random.fold_in(jax.random.fold_in(own_key, 6), dim), (shards_of,), jnp.float32, low / len(cuts), top_value / len(cuts))
        return jnp.repeat(jnp.exp(heights), dims[dim] // shards_of).reshape((-1,) + (1,) * (len(dims) - dim - 1))

    factor_of = one(*cuts[0])
    for cut in cuts[1:]:
        factor_of = factor_of * one(*cut)
    return factor_of


def normal_values(stream_key, extent, width, bound, cuts=(), held_as=jnp.bfloat16):
    level = levels(stream_key, extent, cuts, -0.22, 0.18) if cuts else 1.0
    result = jax.random.normal(stream_key, extent, jnp.float32) * width * level
    return jnp.minimum(jnp.maximum(result, -bound), bound).astype(held_as)


def setup_inputs(seed: int = 0) -> dict:
    key_of = jax.random.split(jax.random.key(seed), 12)
    return {
        "features": normal_values(key_of[0], (VERTS, F), 1.0, 6.0, ((0, 32),)),
        "tile_values": jnp.clip(jnp.exp(math.log(1.0) - 6.9083047 * jax.random.uniform(key_of[1], (N_PROW, N_PCOL, TILES, TILE, TILE), jnp.float32) ** levels(key_of[1], (N_PROW, N_PCOL, TILES, TILE, TILE), ((0, 4), (1, 8)), -0.2, 0.2)), 0.0009994507, 1.0).astype(jnp.bfloat16),
        "tile_rows": draw_tile_rows(jax.random.fold_in(key_of[11], 71), 0),
        "tile_cols": draw_tile_cols(jax.random.fold_in(key_of[11], 71), 0),
        "tile_count": draw_tile_count(jax.random.fold_in(key_of[11], 71), 0),
        "hub_local": draw_hub_local(jax.random.fold_in(key_of[11], 71), 0),
        "hub_edges": jnp.clip(0.5 + 1.5 * jax.random.uniform(key_of[6], (VERTS, HUBS), jnp.float32) ** levels(key_of[6], (VERTS, HUBS), ((0, 32),), -0.2, 0.2), 0.5, 2.0).astype(jnp.bfloat16),
        "w_self": normal_values(key_of[7], (F, F), F ** -0.5, 0.25),
        "w_neigh": normal_values(key_of[8], (F, F), 2.0, 12.0),
        "bias": normal_values(key_of[9], (F,), 0.5, 3.0, (), jnp.float32),
        "cotangent": normal_values(key_of[10], (VERTS, F), 1.0, 6.0, ((0, 32),)),
    }


def reference(features, tile_values, tile_rows, tile_cols, tile_count, hub_local, hub_edges, w_self, w_neigh, bias, cotangent):
    prow_size = N_PROW
    pcol_size = N_PCOL
    part_count = prow_size * pcol_size
    row_tiles = pcol_size * V_DEV // TILE
    col_tiles = prow_size * V_DEV // TILE
    total_rows = part_count * V_DEV
    blocked = features.reshape(prow_size, pcol_size, V_DEV, F)
    tile_flat = tile_values.reshape(part_count, TILES, TILE, TILE)
    row_ids = tile_rows.reshape(part_count, TILES)
    col_ids = tile_cols.reshape(part_count, TILES)
    counts = tile_count.reshape(part_count)
    slot_ids = jnp.arange(TILES, dtype=jnp.int32)

    def forward_part(carry, part_id):
        sum_acc, deg_acc = carry
        row_part = part_id // pcol_size
        col_part = part_id % pcol_size
        source = lax.dynamic_index_in_dim(blocked, col_part, 1, keepdims=False).reshape(col_tiles, TILE, F)
        active = slot_ids < counts[part_id]
        tiles_here = tile_flat[part_id].astype(jnp.float32)
        picked = jnp.take(source, col_ids[part_id], axis=0).astype(jnp.float32)
        product = jnp.einsum('stk,skf->stf', tiles_here, picked)
        product = jnp.where(active[:, None, None], product, jnp.float32(0.0))
        partial_value = jnp.zeros((row_tiles, TILE, F), jnp.float32).at[row_ids[part_id]].add(product)
        row_weight = jnp.where(active[:, None], lax.optimization_barrier(jnp.sum(tiles_here, axis=2)), jnp.float32(0.0))
        partial_deg = jnp.zeros((row_tiles, TILE), jnp.float32).at[row_ids[part_id]].add(row_weight)
        sum_acc = sum_acc.at[row_part].add(partial_value)
        deg_acc = deg_acc.at[row_part].add(partial_deg)
        return ((sum_acc, deg_acc), None)
    start = (jnp.zeros((prow_size, row_tiles, TILE, F), jnp.float32), jnp.zeros((prow_size, row_tiles, TILE), jnp.float32))
    (tile_sums, tile_deg), _ = lax.scan(forward_part, start, jnp.arange(part_count, dtype=jnp.int32))
    hub_features = jnp.take_along_axis(blocked, hub_local[:, :, :, None], axis=2).reshape(HUBS, F)
    hub_sum = jnp.dot(hub_edges, hub_features, preferred_element_type=jnp.float32)
    degree = tile_deg.reshape(total_rows) + lax.optimization_barrier(jnp.sum(hub_edges.astype(jnp.float32), axis=1))
    aggregate = ((tile_sums.reshape(total_rows, F) + hub_sum) / degree[:, None]).astype(jnp.bfloat16)
    pre = jnp.dot(features, w_self, preferred_element_type=jnp.float32) + jnp.dot(aggregate, w_neigh, preferred_element_type=jnp.float32) + bias[None, :]
    sigma = jax.nn.sigmoid(pre)
    activations = (pre * sigma).astype(jnp.bfloat16)
    dpre = cotangent.astype(jnp.float32) * sigma * (1.0 + pre * (1.0 - sigma))
    dpre_b = dpre.astype(jnp.bfloat16)
    factor = 1.0 / math.sqrt(total_rows)
    grad_w_self = jnp.dot(features.T, dpre_b, preferred_element_type=jnp.float32) * factor
    grad_w_neigh = jnp.dot(aggregate.T, dpre_b, preferred_element_type=jnp.float32) * factor
    grad_bias = lax.optimization_barrier(jnp.sum(dpre, axis=0)) * factor
    dagg = jnp.dot(dpre_b, w_neigh.T, preferred_element_type=jnp.float32)
    scaled = (dagg / degree[:, None]).astype(jnp.bfloat16)
    scaled_blocked = scaled.reshape(prow_size, pcol_size, V_DEV, F)

    def backward_part(back_acc, part_id):
        row_part = part_id // pcol_size
        col_part = part_id % pcol_size
        target = lax.dynamic_index_in_dim(scaled_blocked, row_part, 0, keepdims=False).reshape(row_tiles, TILE, F)
        active = slot_ids < counts[part_id]
        tiles_here = tile_flat[part_id].astype(jnp.float32)
        picked = jnp.take(target, row_ids[part_id], axis=0).astype(jnp.float32)
        product = jnp.einsum('stk,stf->skf', tiles_here, picked)
        product = jnp.where(active[:, None, None], product, jnp.float32(0.0))
        partial_value = jnp.zeros((col_tiles, TILE, F), jnp.float32).at[col_ids[part_id]].add(product)
        back_acc = back_acc.at[col_part].add(partial_value)
        return (back_acc, None)
    back_acc, _ = lax.scan(backward_part, jnp.zeros((pcol_size, col_tiles, TILE, F), jnp.float32), jnp.arange(part_count, dtype=jnp.int32))
    back_rows = back_acc.reshape(pcol_size, prow_size, V_DEV, F).transpose(1, 0, 2, 3).reshape(total_rows, F)
    hub_part = jnp.dot(hub_edges.T, scaled, preferred_element_type=jnp.float32).reshape(prow_size, pcol_size, HUB_DEV, F)
    one_hot = (jnp.arange(V_DEV, dtype=jnp.int32)[None, None, :, None] == hub_local[:, :, None, :]).astype(jnp.float32)
    hub_back = jnp.einsum('pqvh,pqhf->pqvf', one_hot, hub_part, precision=lax.Precision.HIGHEST).reshape(total_rows, F)
    grad_features = (jnp.dot(dpre_b, w_self.T, preferred_element_type=jnp.float32) + back_rows + hub_back).astype(jnp.bfloat16)
    return (activations, grad_features, grad_w_self, grad_w_neigh, grad_bias)
```

```python
import math

import jax
import jax.numpy as jnp
from jax import lax
from jax.sharding import PartitionSpec as P


def per_device(
    features,
    tile_values,
    tile_rows,
    tile_cols,
    tile_count,
    hub_local,
    hub_edges,
    w_self,
    w_neigh,
    bias,
    cotangent,
):
    vertex_count, feat_width = features.shape
    tile_edge = tile_values.shape[-1]
    slot_count = tile_values.shape[2]
    hub_count = hub_local.shape[-1]
    prow_size = lax.axis_size("prow")
    pcol_size = lax.axis_size("pcol")
    row_tiles = pcol_size * vertex_count // tile_edge
    col_tiles = prow_size * vertex_count // tile_edge
    positions = row_tiles * col_tiles

    tiles = tile_values.reshape(slot_count, tile_edge, tile_edge)
    live = jnp.arange(slot_count, dtype=jnp.int32) < tile_count.reshape(())
    pos = tile_rows.reshape(slot_count) * col_tiles + tile_cols.reshape(slot_count)
    place = (pos[:, None] == jnp.arange(positions, dtype=jnp.int32)[None, :]) & live[:, None]
    dense = jnp.einsum(
        "sp,sab->pab", place.astype(jnp.bfloat16), tiles, preferred_element_type=jnp.bfloat16
    )
    adj = (
        dense.reshape(row_tiles, col_tiles, tile_edge, tile_edge)
        .transpose(0, 2, 1, 3)
        .reshape(row_tiles * tile_edge, col_tiles * tile_edge)
    )

    hub_ids = hub_local.reshape(hub_count)
    hub_rows = jnp.take(features, hub_ids, axis=0)
    payload = jnp.concatenate([features, hub_rows], axis=0)
    gathered = lax.all_gather(payload, "prow", axis=0, tiled=False)
    source_cols = gathered[:, :vertex_count].reshape(prow_size * vertex_count, feat_width)
    hub_col = gathered[:, vertex_count:]
    hub_all = lax.all_gather(
        hub_col.reshape(prow_size * hub_count, feat_width), "pcol", axis=0, tiled=True
    )
    hub_features = (
        hub_all.reshape(pcol_size, prow_size, hub_count, feat_width)
        .transpose(1, 0, 2, 3)
        .reshape(prow_size * pcol_size * hub_count, feat_width)
    )

    row_sums = jnp.dot(adj, source_cols, preferred_element_type=jnp.float32)
    row_deg = jnp.sum(adj, axis=1, dtype=jnp.float32)
    deg_row = jnp.pad(
        row_deg.reshape(pcol_size, 1, vertex_count), ((0, 0), (0, 0), (0, feat_width - vertex_count))
    )
    packed = jnp.concatenate(
        [row_sums.reshape(pcol_size, vertex_count, feat_width), deg_row], axis=1
    )
    reduced = lax.psum_scatter(packed, "pcol", scatter_dimension=0, tiled=True)
    own_sums = reduced[0, :vertex_count]
    own_deg = reduced[0, vertex_count, :vertex_count]

    hub_sum = jnp.dot(hub_edges, hub_features, preferred_element_type=jnp.float32)
    degree = own_deg + jnp.sum(hub_edges, axis=1, dtype=jnp.float32)
    aggregate = ((own_sums + hub_sum) / degree[:, None]).astype(jnp.bfloat16)
    pre = (
        jnp.dot(features, w_self, preferred_element_type=jnp.float32)
        + jnp.dot(aggregate, w_neigh, preferred_element_type=jnp.float32)
        + bias[None, :]
    )
    sigma = jax.nn.sigmoid(pre)
    activations = (pre * sigma).astype(jnp.bfloat16)
    dpre = cotangent.astype(jnp.float32) * sigma * (1.0 + pre * (1.0 - sigma))
    dpre_b = dpre.astype(jnp.bfloat16)
    total_rows = prow_size * pcol_size * vertex_count
    factor = 1.0 / math.sqrt(total_rows)
    self_part = jnp.dot(features.T, dpre_b, preferred_element_type=jnp.float32)
    neigh_part = jnp.dot(aggregate.T, dpre_b, preferred_element_type=jnp.float32)
    bias_part = jnp.sum(dpre, axis=0)
    grad_pack = jnp.concatenate(
        [
            self_part,
            neigh_part,
            jnp.broadcast_to(bias_part[None, :], (8, feat_width)),
        ],
        axis=0,
    )
    grad_total = lax.psum(grad_pack, ("prow", "pcol"))
    grad_w_self = grad_total[:feat_width] * factor
    grad_w_neigh = grad_total[feat_width : 2 * feat_width] * factor
    grad_bias = grad_total[2 * feat_width] * factor

    dagg = jnp.dot(dpre_b, w_neigh.T, preferred_element_type=jnp.float32)
    scaled = (dagg / degree[:, None]).astype(jnp.bfloat16)
    target_rows = lax.all_gather(scaled, "pcol", axis=0, tiled=True)
    back = lax.dot_general(
        adj, target_rows, (((0,), (0,)), ((), ())), preferred_element_type=jnp.float32
    )

    hub_part = jnp.dot(hub_edges.T, scaled, preferred_element_type=jnp.float32)
    hub_by_col = hub_part.reshape(prow_size, pcol_size, hub_count, feat_width).transpose(1, 0, 2, 3)
    hub_col_sum = lax.psum_scatter(hub_by_col, "pcol", scatter_dimension=0, tiled=True)
    back_ext = jnp.concatenate(
        [
            back.reshape(prow_size, vertex_count, feat_width),
            hub_col_sum.reshape(prow_size, hub_count, feat_width),
        ],
        axis=1,
    ).astype(jnp.bfloat16)
    back_own = lax.psum_scatter(back_ext, "prow", scatter_dimension=0, tiled=True)
    back_rows = back_own[0, :vertex_count].astype(jnp.float32)
    own_hubs = back_own[0, vertex_count:]
    one_hot = (jnp.arange(vertex_count, dtype=jnp.int32)[:, None] == hub_ids[None, :]).astype(
        jnp.bfloat16
    )
    hub_back = jnp.dot(one_hot, own_hubs, preferred_element_type=jnp.float32)
    grad_features = (
        jnp.dot(dpre_b, w_self.T, preferred_element_type=jnp.float32) + back_rows + hub_back
    ).astype(jnp.bfloat16)
    return (activations, grad_features, grad_w_self, grad_w_neigh, grad_bias)


def solution(mesh):
    in_specs = (
        P(("prow", "pcol"), None),
        P("prow", "pcol", None, None, None),
        P("prow", "pcol", None),
        P("prow", "pcol", None),
        P("prow", "pcol"),
        P("prow", "pcol", None),
        P(("prow", "pcol"), None),
        P(),
        P(),
        P(),
        P(("prow", "pcol"), None),
    )
    out_specs = (P(("prow", "pcol"), None), P(("prow", "pcol"), None), P(), P(), P())
    return jax.shard_map(
        per_device, mesh=mesh, in_specs=in_specs, out_specs=out_specs, check_vma=False
    )
```

```python
import math

import jax
import jax.numpy as jnp
from jax import lax
from jax.sharding import PartitionSpec as P


def _pairwise_allreduce(flat, axes):
    steps = []
    for axis in axes:
        size = lax.axis_size(axis)
        bit = 1
        while bit < size:
            steps.append((axis, size, bit))
            bit *= 2
    x = flat
    for axis, size, bit in steps:
        upper = (lax.axis_index(axis) // bit) % 2 == 1
        half = x.shape[0] // 2
        low, high = x[:half], x[half:]
        keep = jnp.where(upper, high, low)
        send = jnp.where(upper, low, high)
        perm = [(k, k ^ bit) for k in range(size)]
        x = keep + lax.ppermute(send, axis, perm)
    for axis, size, bit in reversed(steps):
        upper = (lax.axis_index(axis) // bit) % 2 == 1
        perm = [(k, k ^ bit) for k in range(size)]
        other = lax.ppermute(x, axis, perm)
        x = jnp.where(upper, jnp.concatenate([other, x]), jnp.concatenate([x, other]))
    return x


def per_device(
    features,
    tile_values,
    tile_rows,
    tile_cols,
    tile_count,
    hub_local,
    hub_edges,
    w_self,
    w_neigh,
    bias,
    cotangent,
):
    vertex_count, feat_width = features.shape
    tile_edge = tile_values.shape[-1]
    slot_count = tile_values.shape[2]
    hub_count = hub_local.shape[-1]
    prow_size = lax.axis_size("prow")
    pcol_size = lax.axis_size("pcol")
    row_tiles = pcol_size * vertex_count // tile_edge
    col_tiles = prow_size * vertex_count // tile_edge
    positions = row_tiles * col_tiles

    tiles = tile_values.reshape(slot_count, tile_edge, tile_edge)
    live = jnp.arange(slot_count, dtype=jnp.int32) < tile_count.reshape(())
    pos = tile_rows.reshape(slot_count) * col_tiles + tile_cols.reshape(slot_count)
    place = (pos[:, None] == jnp.arange(positions, dtype=jnp.int32)[None, :]) & live[:, None]
    dense = jnp.einsum(
        "sp,sab->pab", place.astype(jnp.bfloat16), tiles, preferred_element_type=jnp.bfloat16
    )
    adj = (
        dense.reshape(row_tiles, col_tiles, tile_edge, tile_edge)
        .transpose(0, 2, 1, 3)
        .reshape(row_tiles * tile_edge, col_tiles * tile_edge)
    )

    hub_ids = hub_local.reshape(hub_count)
    hub_rows = jnp.take(features, hub_ids, axis=0)
    payload = jnp.concatenate([features, hub_rows], axis=0)
    gathered = lax.all_gather(payload, "prow", axis=0, tiled=False)
    source_cols = gathered[:, :vertex_count].reshape(prow_size * vertex_count, feat_width)
    hub_col = gathered[:, vertex_count:]
    hub_all = lax.all_gather(
        hub_col.reshape(prow_size * hub_count, feat_width), "pcol", axis=0, tiled=True
    )
    hub_features = (
        hub_all.reshape(pcol_size, prow_size, hub_count, feat_width)
        .transpose(1, 0, 2, 3)
        .reshape(prow_size * pcol_size * hub_count, feat_width)
    )

    edges_by_col = hub_edges.reshape(vertex_count, prow_size, pcol_size, hub_count).transpose(
        2, 0, 1, 3
    )
    hub_cols = lax.all_to_all(edges_by_col, "pcol", 0, 0, tiled=True).reshape(
        pcol_size * vertex_count, prow_size * hub_count
    )

    row_sums = jnp.dot(adj, source_cols, preferred_element_type=jnp.float32)
    row_deg = jnp.sum(adj, axis=1, dtype=jnp.float32)
    deg_row = jnp.pad(
        row_deg.reshape(pcol_size, 1, vertex_count), ((0, 0), (0, 0), (0, feat_width - vertex_count))
    )
    packed = jnp.concatenate(
        [row_sums.reshape(pcol_size, vertex_count, feat_width), deg_row], axis=1
    )
    reduced = lax.psum_scatter(packed, "pcol", scatter_dimension=0, tiled=True)
    own_sums = reduced[0, :vertex_count]
    own_deg = reduced[0, vertex_count, :vertex_count]

    hub_sum = jnp.dot(hub_edges, hub_features, preferred_element_type=jnp.float32)
    degree = own_deg + jnp.sum(hub_edges, axis=1, dtype=jnp.float32)
    aggregate = ((own_sums + hub_sum) / degree[:, None]).astype(jnp.bfloat16)
    pre = (
        jnp.dot(features, w_self, preferred_element_type=jnp.float32)
        + jnp.dot(aggregate, w_neigh, preferred_element_type=jnp.float32)
        + bias[None, :]
    )
    sigma = jax.nn.sigmoid(pre)
    activations = (pre * sigma).astype(jnp.bfloat16)
    dpre = cotangent.astype(jnp.float32) * sigma * (1.0 + pre * (1.0 - sigma))
    dpre_b = dpre.astype(jnp.bfloat16)
    total_rows = prow_size * pcol_size * vertex_count
    factor = 1.0 / math.sqrt(total_rows)
    self_part = jnp.dot(features.T, dpre_b, preferred_element_type=jnp.float32)
    neigh_part = jnp.dot(aggregate.T, dpre_b, preferred_element_type=jnp.float32)
    bias_part = jnp.sum(dpre, axis=0)
    grad_pack = jnp.concatenate(
        [
            self_part,
            neigh_part,
            jnp.broadcast_to(bias_part[None, :], (8, feat_width)),
        ],
        axis=0,
    )
    grad_total = _pairwise_allreduce(grad_pack.reshape(-1), ("prow", "pcol")).reshape(
        grad_pack.shape
    )
    grad_w_self = grad_total[:feat_width] * factor
    grad_w_neigh = grad_total[feat_width : 2 * feat_width] * factor
    grad_bias = grad_total[2 * feat_width] * factor

    dagg = jnp.dot(dpre_b, w_neigh.T, preferred_element_type=jnp.float32)
    scaled = (dagg / degree[:, None]).astype(jnp.bfloat16)
    target_rows = lax.all_gather(scaled, "pcol", axis=0, tiled=True)
    back = lax.dot_general(
        adj, target_rows, (((0,), (0,)), ((), ())), preferred_element_type=jnp.float32
    )

    hub_col_sum = lax.dot_general(
        hub_cols, target_rows, (((0,), (0,)), ((), ())), preferred_element_type=jnp.float32
    )
    back_ext = jnp.concatenate(
        [
            back.reshape(prow_size, vertex_count, feat_width),
            hub_col_sum.reshape(prow_size, hub_count, feat_width),
        ],
        axis=1,
    ).astype(jnp.bfloat16)
    back_own = lax.psum_scatter(back_ext, "prow", scatter_dimension=0, tiled=True)
    back_rows = back_own[0, :vertex_count].astype(jnp.float32)
    own_hubs = back_own[0, vertex_count:]
    one_hot = (jnp.arange(vertex_count, dtype=jnp.int32)[:, None] == hub_ids[None, :]).astype(
        jnp.bfloat16
    )
    hub_back = jnp.dot(one_hot, own_hubs, preferred_element_type=jnp.float32)
    grad_features = (
        jnp.dot(dpre_b, w_self.T, preferred_element_type=jnp.float32) + back_rows + hub_back
    ).astype(jnp.bfloat16)
    return (activations, grad_features, grad_w_self, grad_w_neigh, grad_bias)


def solution(mesh):
    in_specs = (
        P(("prow", "pcol"), None),
        P("prow", "pcol", None, None, None),
        P("prow", "pcol", None),
        P("prow", "pcol", None),
        P("prow", "pcol"),
        P("prow", "pcol", None),
        P(("prow", "pcol"), None),
        P(),
        P(),
        P(),
        P(("prow", "pcol"), None),
    )
    out_specs = (P(("prow", "pcol"), None), P(("prow", "pcol"), None), P(), P(), P())
    return jax.shard_map(
        per_device, mesh=mesh, in_specs=in_specs, out_specs=out_specs, check_vma=False
    )
```

```python
import math

import jax
import jax.numpy as jnp
from jax import lax
from jax.sharding import PartitionSpec as P


def _pairwise_allreduce(flat, axes):
    steps = []
    for axis in axes:
        size = lax.axis_size(axis)
        bit = 1
        while bit < size:
            steps.append((axis, size, bit))
            bit *= 2
    x = flat
    for axis, size, bit in steps:
        upper = (lax.axis_index(axis) // bit) % 2 == 1
        half = x.shape[0] // 2
        low, high = x[:half], x[half:]
        keep = jnp.where(upper, high, low)
        send = jnp.where(upper, low, high)
        perm = [(k, k ^ bit) for k in range(size)]
        x = keep + lax.ppermute(send, axis, perm)
    for axis, size, bit in reversed(steps):
        upper = (lax.axis_index(axis) // bit) % 2 == 1
        perm = [(k, k ^ bit) for k in range(size)]
        other = lax.ppermute(x, axis, perm)
        x = jnp.where(upper, jnp.concatenate([other, x]), jnp.concatenate([x, other]))
    return x


def per_device(
    features,
    tile_values,
    tile_rows,
    tile_cols,
    tile_count,
    hub_local,
    hub_edges,
    w_self,
    w_neigh,
    bias,
    cotangent,
):
    vertex_count, feat_width = features.shape
    tile_edge = tile_values.shape[-1]
    slot_count = tile_values.shape[2]
    hub_count = hub_local.shape[-1]
    prow_size = lax.axis_size("prow")
    pcol_size = lax.axis_size("pcol")
    row_tiles = pcol_size * vertex_count // tile_edge
    col_tiles = prow_size * vertex_count // tile_edge
    positions = row_tiles * col_tiles

    tiles = tile_values.reshape(slot_count, tile_edge, tile_edge)
    live = jnp.arange(slot_count, dtype=jnp.int32) < tile_count.reshape(())
    pos = tile_rows.reshape(slot_count) * col_tiles + tile_cols.reshape(slot_count)
    place = (pos[:, None] == jnp.arange(positions, dtype=jnp.int32)[None, :]) & live[:, None]
    dense = jnp.einsum(
        "sp,sab->pab", place.astype(jnp.bfloat16), tiles, preferred_element_type=jnp.bfloat16
    )
    adj = (
        dense.reshape(row_tiles, col_tiles, tile_edge, tile_edge)
        .transpose(0, 2, 1, 3)
        .reshape(row_tiles * tile_edge, col_tiles * tile_edge)
    )

    hub_ids = hub_local.reshape(hub_count)
    hub_rows = jnp.take(features, hub_ids, axis=0)
    payload = jnp.concatenate([features, hub_rows], axis=0)
    gathered = lax.all_gather(payload, "prow", axis=0, tiled=False)
    source_cols = gathered[:, :vertex_count].reshape(prow_size * vertex_count, feat_width)
    hub_col = gathered[:, vertex_count:]
    hub_all = lax.all_gather(
        hub_col.reshape(prow_size * hub_count, feat_width), "pcol", axis=0, tiled=True
    )
    hub_features = (
        hub_all.reshape(pcol_size, prow_size, hub_count, feat_width)
        .transpose(1, 0, 2, 3)
        .reshape(prow_size * pcol_size * hub_count, feat_width)
    )

    edges_by_col = hub_edges.reshape(vertex_count, prow_size, pcol_size, hub_count).transpose(
        2, 0, 1, 3
    )
    hub_cols = lax.all_to_all(edges_by_col, "pcol", 0, 0, tiled=True).reshape(
        pcol_size * vertex_count, prow_size * hub_count
    )

    row_sums = jnp.dot(adj, source_cols, preferred_element_type=jnp.float32)
    row_deg = jnp.sum(adj, axis=1, dtype=jnp.float32)
    deg_row = jnp.pad(
        row_deg.reshape(pcol_size, 1, vertex_count), ((0, 0), (0, 0), (0, feat_width - vertex_count))
    )
    packed = jnp.concatenate(
        [row_sums.reshape(pcol_size, vertex_count, feat_width), deg_row], axis=1
    )
    reduced = lax.psum_scatter(packed, "pcol", scatter_dimension=0, tiled=True)
    own_sums = reduced[0, :vertex_count]
    own_deg = reduced[0, vertex_count, :vertex_count]

    hub_sum = jnp.dot(hub_edges, hub_features, preferred_element_type=jnp.float32)
    degree = own_deg + jnp.sum(hub_edges, axis=1, dtype=jnp.float32)
    aggregate = ((own_sums + hub_sum) / degree[:, None]).astype(jnp.bfloat16)
    pre = (
        jnp.dot(features, w_self, preferred_element_type=jnp.float32)
        + jnp.dot(aggregate, w_neigh, preferred_element_type=jnp.float32)
        + bias[None, :]
    )
    sigma = jax.nn.sigmoid(pre)
    activations = (pre * sigma).astype(jnp.bfloat16)
    dpre = cotangent.astype(jnp.float32) * sigma * (1.0 + pre * (1.0 - sigma))
    dpre_b = dpre.astype(jnp.bfloat16)
    total_rows = prow_size * pcol_size * vertex_count
    factor = 1.0 / math.sqrt(total_rows)
    dagg = jnp.dot(dpre_b, w_neigh.T, preferred_element_type=jnp.float32)
    scaled = (dagg / degree[:, None]).astype(jnp.bfloat16)
    scaled, dpre, dpre_b, aggregate = lax.optimization_barrier((scaled, dpre, dpre_b, aggregate))
    self_part = jnp.dot(features.T, dpre_b, preferred_element_type=jnp.float32)
    neigh_part = jnp.dot(aggregate.T, dpre_b, preferred_element_type=jnp.float32)
    bias_part = jnp.sum(dpre, axis=0)
    grad_pack = jnp.concatenate(
        [
            self_part,
            neigh_part,
            jnp.broadcast_to(bias_part[None, :], (8, feat_width)),
        ],
        axis=0,
    )
    grad_total = _pairwise_allreduce(grad_pack.reshape(-1), ("prow", "pcol")).reshape(
        grad_pack.shape
    )
    grad_w_self = grad_total[:feat_width] * factor
    grad_w_neigh = grad_total[feat_width : 2 * feat_width] * factor
    grad_bias = grad_total[2 * feat_width] * factor

    target_rows = lax.all_gather(scaled, "pcol", axis=0, tiled=True)
    back = lax.dot_general(
        adj, target_rows, (((0,), (0,)), ((), ())), preferred_element_type=jnp.float32
    )

    hub_col_sum = lax.dot_general(
        hub_cols, target_rows, (((0,), (0,)), ((), ())), preferred_element_type=jnp.float32
    )
    back_ext = jnp.concatenate(
        [
            back.reshape(prow_size, vertex_count, feat_width),
            hub_col_sum.reshape(prow_size, hub_count, feat_width),
        ],
        axis=1,
    ).astype(jnp.bfloat16)
    back_own = lax.psum_scatter(back_ext, "prow", scatter_dimension=0, tiled=True)
    back_rows = back_own[0, :vertex_count].astype(jnp.float32)
    own_hubs = back_own[0, vertex_count:]
    one_hot = (jnp.arange(vertex_count, dtype=jnp.int32)[:, None] == hub_ids[None, :]).astype(
        jnp.bfloat16
    )
    hub_back = jnp.dot(one_hot, own_hubs, preferred_element_type=jnp.float32)
    grad_features = (
        jnp.dot(dpre_b, w_self.T, preferred_element_type=jnp.float32) + back_rows + hub_back
    ).astype(jnp.bfloat16)
    return (activations, grad_features, grad_w_self, grad_w_neigh, grad_bias)


def solution(mesh):
    in_specs = (
        P(("prow", "pcol"), None),
        P("prow", "pcol", None, None, None),
        P("prow", "pcol", None),
        P("prow", "pcol", None),
        P("prow", "pcol"),
        P("prow", "pcol", None),
        P(("prow", "pcol"), None),
        P(),
        P(),
        P(),
        P(("prow", "pcol"), None),
    )
    out_specs = (P(("prow", "pcol"), None), P(("prow", "pcol"), None), P(), P(), P())
    return jax.shard_map(
        per_device, mesh=mesh, in_specs=in_specs, out_specs=out_specs, check_vma=False
    )
```

```python
import math

import jax
import jax.numpy as jnp
from jax import lax
from jax.sharding import PartitionSpec as P


def _pairwise_allreduce(flat, axes):
    steps = []
    for axis in axes:
        size = lax.axis_size(axis)
        bit = 1
        while bit < size:
            steps.append((axis, size, bit))
            bit *= 2
    x = flat
    for axis, size, bit in steps:
        upper = (lax.axis_index(axis) // bit) % 2 == 1
        half = x.shape[0] // 2
        low, high = x[:half], x[half:]
        keep = jnp.where(upper, high, low)
        send = jnp.where(upper, low, high)
        perm = [(k, k ^ bit) for k in range(size)]
        x = keep + lax.ppermute(send, axis, perm)
    for axis, size, bit in reversed(steps):
        upper = (lax.axis_index(axis) // bit) % 2 == 1
        perm = [(k, k ^ bit) for k in range(size)]
        other = lax.ppermute(x, axis, perm)
        x = jnp.where(upper, jnp.concatenate([other, x]), jnp.concatenate([x, other]))
    return x


def per_device(
    features,
    tile_values,
    tile_rows,
    tile_cols,
    tile_count,
    hub_local,
    hub_edges,
    w_self,
    w_neigh,
    bias,
    cotangent,
):
    vertex_count, feat_width = features.shape
    tile_edge = tile_values.shape[-1]
    slot_count = tile_values.shape[2]
    hub_count = hub_local.shape[-1]
    prow_size = lax.axis_size("prow")
    pcol_size = lax.axis_size("pcol")
    row_tiles = pcol_size * vertex_count // tile_edge
    col_tiles = prow_size * vertex_count // tile_edge
    positions = row_tiles * col_tiles

    tiles = tile_values.reshape(slot_count, tile_edge, tile_edge)
    live = jnp.arange(slot_count, dtype=jnp.int32) < tile_count.reshape(())
    pos = tile_rows.reshape(slot_count) * col_tiles + tile_cols.reshape(slot_count)
    place = (pos[:, None] == jnp.arange(positions, dtype=jnp.int32)[None, :]) & live[:, None]
    dense = jnp.einsum(
        "sp,sab->pab", place.astype(jnp.bfloat16), tiles, preferred_element_type=jnp.bfloat16
    )
    adj = (
        dense.reshape(row_tiles, col_tiles, tile_edge, tile_edge)
        .transpose(0, 2, 1, 3)
        .reshape(row_tiles * tile_edge, col_tiles * tile_edge)
    )

    hub_ids = hub_local.reshape(hub_count)
    hub_rows = jnp.take(features, hub_ids, axis=0)
    payload = jnp.concatenate([features, hub_rows], axis=0)
    gathered = lax.all_gather(payload, "prow", axis=0, tiled=False)
    source_cols = gathered[:, :vertex_count].reshape(prow_size * vertex_count, feat_width)
    hub_col = gathered[:, vertex_count:]
    hub_all = lax.all_gather(
        hub_col.reshape(prow_size * hub_count, feat_width), "pcol", axis=0, tiled=True
    )
    hub_features = (
        hub_all.reshape(pcol_size, prow_size, hub_count, feat_width)
        .transpose(1, 0, 2, 3)
        .reshape(prow_size * pcol_size * hub_count, feat_width)
    )

    edges_by_col = hub_edges.reshape(vertex_count, prow_size, pcol_size, hub_count).transpose(
        2, 0, 1, 3
    )
    hub_cols = lax.all_to_all(edges_by_col, "pcol", 0, 0, tiled=True).reshape(
        pcol_size * vertex_count, prow_size * hub_count
    )

    row_sums = jnp.dot(adj, source_cols, preferred_element_type=jnp.float32)
    row_deg = jnp.sum(adj, axis=1, dtype=jnp.float32)
    deg_row = jnp.pad(
        row_deg.reshape(pcol_size, 1, vertex_count), ((0, 0), (0, 0), (0, feat_width - vertex_count))
    )
    packed = jnp.concatenate(
        [row_sums.reshape(pcol_size, vertex_count, feat_width), deg_row], axis=1
    )
    reduced = lax.psum_scatter(
        packed.astype(jnp.bfloat16), "pcol", scatter_dimension=0, tiled=True
    ).astype(jnp.float32)
    own_sums = reduced[0, :vertex_count]
    own_deg = reduced[0, vertex_count, :vertex_count]

    hub_sum = jnp.dot(hub_edges, hub_features, preferred_element_type=jnp.float32)
    degree = own_deg + jnp.sum(hub_edges, axis=1, dtype=jnp.float32)
    aggregate = ((own_sums + hub_sum) / degree[:, None]).astype(jnp.bfloat16)
    pre = (
        jnp.dot(features, w_self, preferred_element_type=jnp.float32)
        + jnp.dot(aggregate, w_neigh, preferred_element_type=jnp.float32)
        + bias[None, :]
    )
    sigma = jax.nn.sigmoid(pre)
    activations = (pre * sigma).astype(jnp.bfloat16)
    dpre = cotangent.astype(jnp.float32) * sigma * (1.0 + pre * (1.0 - sigma))
    dpre_b = dpre.astype(jnp.bfloat16)
    total_rows = prow_size * pcol_size * vertex_count
    factor = 1.0 / math.sqrt(total_rows)
    dagg = jnp.dot(dpre_b, w_neigh.T, preferred_element_type=jnp.float32)
    scaled = (dagg / degree[:, None]).astype(jnp.bfloat16)
    scaled, dpre, dpre_b, aggregate = lax.optimization_barrier((scaled, dpre, dpre_b, aggregate))
    self_part = jnp.dot(features.T, dpre_b, preferred_element_type=jnp.float32)
    neigh_part = jnp.dot(aggregate.T, dpre_b, preferred_element_type=jnp.float32)
    bias_part = jnp.sum(dpre, axis=0)
    grad_pack = jnp.concatenate(
        [
            self_part,
            neigh_part,
            jnp.broadcast_to(bias_part[None, :], (8, feat_width)),
        ],
        axis=0,
    )
    grad_total = _pairwise_allreduce(grad_pack.reshape(-1), ("prow", "pcol")).reshape(
        grad_pack.shape
    )
    grad_w_self = grad_total[:feat_width] * factor
    grad_w_neigh = grad_total[feat_width : 2 * feat_width] * factor
    grad_bias = grad_total[2 * feat_width] * factor

    target_rows = lax.all_gather(scaled, "pcol", axis=0, tiled=True)
    back = lax.dot_general(
        adj, target_rows, (((0,), (0,)), ((), ())), preferred_element_type=jnp.float32
    )

    hub_col_sum = lax.dot_general(
        hub_cols, target_rows, (((0,), (0,)), ((), ())), preferred_element_type=jnp.float32
    )
    back_ext = jnp.concatenate(
        [
            back.reshape(prow_size, vertex_count, feat_width),
            hub_col_sum.reshape(prow_size, hub_count, feat_width),
        ],
        axis=1,
    ).astype(jnp.bfloat16)
    back_own = lax.psum_scatter(back_ext, "prow", scatter_dimension=0, tiled=True)
    back_rows = back_own[0, :vertex_count].astype(jnp.float32)
    own_hubs = back_own[0, vertex_count:]
    one_hot = (jnp.arange(vertex_count, dtype=jnp.int32)[:, None] == hub_ids[None, :]).astype(
        jnp.bfloat16
    )
    hub_back = jnp.dot(one_hot, own_hubs, preferred_element_type=jnp.float32)
    grad_features = (
        jnp.dot(dpre_b, w_self.T, preferred_element_type=jnp.float32) + back_rows + hub_back
    ).astype(jnp.bfloat16)
    return (activations, grad_features, grad_w_self, grad_w_neigh, grad_bias)


def solution(mesh):
    in_specs = (
        P(("prow", "pcol"), None),
        P("prow", "pcol", None, None, None),
        P("prow", "pcol", None),
        P("prow", "pcol", None),
        P("prow", "pcol"),
        P("prow", "pcol", None),
        P(("prow", "pcol"), None),
        P(),
        P(),
        P(),
        P(("prow", "pcol"), None),
    )
    out_specs = (P(("prow", "pcol"), None), P(("prow", "pcol"), None), P(), P(), P())
    return jax.shard_map(
        per_device, mesh=mesh, in_specs=in_specs, out_specs=out_specs, check_vma=False
    )
```

```python
import math

import jax
import jax.numpy as jnp
from jax import lax
from jax.sharding import PartitionSpec as P


def _pairwise_allreduce(flat, axes):
    steps = []
    for axis in axes:
        size = lax.axis_size(axis)
        bit = 1
        while bit < size:
            steps.append((axis, size, bit))
            bit *= 2
    x = flat
    for axis, size, bit in steps:
        upper = (lax.axis_index(axis) // bit) % 2 == 1
        half = x.shape[0] // 2
        low, high = x[:half], x[half:]
        keep = jnp.where(upper, high, low)
        send = jnp.where(upper, low, high)
        perm = [(k, k ^ bit) for k in range(size)]
        x = keep + lax.ppermute(send, axis, perm)
    for axis, size, bit in reversed(steps):
        upper = (lax.axis_index(axis) // bit) % 2 == 1
        perm = [(k, k ^ bit) for k in range(size)]
        other = lax.ppermute(x, axis, perm)
        x = jnp.where(upper, jnp.concatenate([other, x]), jnp.concatenate([x, other]))
    return x


def per_device(
    features,
    tile_values,
    tile_rows,
    tile_cols,
    tile_count,
    hub_local,
    hub_edges,
    w_self,
    w_neigh,
    bias,
    cotangent,
):
    vertex_count, feat_width = features.shape
    tile_edge = tile_values.shape[-1]
    slot_count = tile_values.shape[2]
    hub_count = hub_local.shape[-1]
    prow_size = lax.axis_size("prow")
    pcol_size = lax.axis_size("pcol")
    row_tiles = pcol_size * vertex_count // tile_edge
    col_tiles = prow_size * vertex_count // tile_edge
    positions = row_tiles * col_tiles

    tiles = tile_values.reshape(slot_count, tile_edge, tile_edge)
    live = jnp.arange(slot_count, dtype=jnp.int32) < tile_count.reshape(())
    pos = tile_rows.reshape(slot_count) * col_tiles + tile_cols.reshape(slot_count)
    place = (pos[:, None] == jnp.arange(positions, dtype=jnp.int32)[None, :]) & live[:, None]
    dense = jnp.einsum(
        "sp,sab->pab", place.astype(jnp.bfloat16), tiles, preferred_element_type=jnp.bfloat16
    )
    adj = (
        dense.reshape(row_tiles, col_tiles, tile_edge, tile_edge)
        .transpose(0, 2, 1, 3)
        .reshape(row_tiles * tile_edge, col_tiles * tile_edge)
    )

    hub_ids = hub_local.reshape(hub_count)
    hub_rows = jnp.take(features, hub_ids, axis=0)
    payload = jnp.concatenate([features, hub_rows], axis=0)
    gathered = lax.all_gather(payload, "prow", axis=0, tiled=False)
    source_cols = gathered[:, :vertex_count].reshape(prow_size * vertex_count, feat_width)
    hub_col = gathered[:, vertex_count:]
    hub_all = lax.all_gather(
        hub_col.reshape(prow_size * hub_count, feat_width), "pcol", axis=0, tiled=True
    )
    hub_features = (
        hub_all.reshape(pcol_size, prow_size, hub_count, feat_width)
        .transpose(1, 0, 2, 3)
        .reshape(prow_size * pcol_size * hub_count, feat_width)
    )

    edges_by_col = hub_edges.reshape(vertex_count, prow_size, pcol_size, hub_count).transpose(
        2, 0, 1, 3
    )
    hub_cols = lax.all_to_all(edges_by_col, "pcol", 0, 0, tiled=True).reshape(
        pcol_size * vertex_count, prow_size * hub_count
    )

    row_sums = jnp.dot(adj, source_cols, preferred_element_type=jnp.float32)
    row_deg = jnp.sum(adj, axis=1, dtype=jnp.float32)
    deg_row = jnp.pad(
        row_deg.reshape(pcol_size, 1, vertex_count), ((0, 0), (0, 0), (0, feat_width - vertex_count))
    )
    packed = jnp.concatenate(
        [row_sums.reshape(pcol_size, vertex_count, feat_width), deg_row], axis=1
    )
    reduced = jnp.sum(lax.all_to_all(packed, "pcol", 0, 0, tiled=True), axis=0)
    own_sums = reduced[:vertex_count]
    own_deg = reduced[vertex_count, :vertex_count]

    hub_sum = jnp.dot(hub_edges, hub_features, preferred_element_type=jnp.float32)
    degree = own_deg + jnp.sum(hub_edges, axis=1, dtype=jnp.float32)
    aggregate = ((own_sums + hub_sum) / degree[:, None]).astype(jnp.bfloat16)
    pre = (
        jnp.dot(features, w_self, preferred_element_type=jnp.float32)
        + jnp.dot(aggregate, w_neigh, preferred_element_type=jnp.float32)
        + bias[None, :]
    )
    sigma = jax.nn.sigmoid(pre)
    activations = (pre * sigma).astype(jnp.bfloat16)
    dpre = cotangent.astype(jnp.float32) * sigma * (1.0 + pre * (1.0 - sigma))
    dpre_b = dpre.astype(jnp.bfloat16)
    total_rows = prow_size * pcol_size * vertex_count
    factor = 1.0 / math.sqrt(total_rows)
    dagg = jnp.dot(dpre_b, w_neigh.T, preferred_element_type=jnp.float32)
    scaled = (dagg / degree[:, None]).astype(jnp.bfloat16)
    scaled, dpre, dpre_b, aggregate = lax.optimization_barrier((scaled, dpre, dpre_b, aggregate))
    self_part = jnp.dot(features.T, dpre_b, preferred_element_type=jnp.float32)
    neigh_part = jnp.dot(aggregate.T, dpre_b, preferred_element_type=jnp.float32)
    bias_part = jnp.sum(dpre, axis=0)
    grad_pack = jnp.concatenate(
        [
            self_part,
            neigh_part,
            jnp.broadcast_to(bias_part[None, :], (8, feat_width)),
        ],
        axis=0,
    )
    grad_total = _pairwise_allreduce(grad_pack.reshape(-1), ("prow", "pcol")).reshape(
        grad_pack.shape
    )
    grad_w_self = grad_total[:feat_width] * factor
    grad_w_neigh = grad_total[feat_width : 2 * feat_width] * factor
    grad_bias = grad_total[2 * feat_width] * factor

    target_rows = lax.all_gather(scaled, "pcol", axis=0, tiled=True)
    back = lax.dot_general(
        adj, target_rows, (((0,), (0,)), ((), ())), preferred_element_type=jnp.float32
    )

    hub_col_sum = lax.dot_general(
        hub_cols, target_rows, (((0,), (0,)), ((), ())), preferred_element_type=jnp.float32
    )
    back_ext = jnp.concatenate(
        [
            back.reshape(prow_size, vertex_count, feat_width),
            hub_col_sum.reshape(prow_size, hub_count, feat_width),
        ],
        axis=1,
    ).astype(jnp.bfloat16)
    back_own = lax.psum_scatter(back_ext, "prow", scatter_dimension=0, tiled=True)
    back_rows = back_own[0, :vertex_count].astype(jnp.float32)
    own_hubs = back_own[0, vertex_count:]
    one_hot = (jnp.arange(vertex_count, dtype=jnp.int32)[:, None] == hub_ids[None, :]).astype(
        jnp.bfloat16
    )
    hub_back = jnp.dot(one_hot, own_hubs, preferred_element_type=jnp.float32)
    grad_features = (
        jnp.dot(dpre_b, w_self.T, preferred_element_type=jnp.float32) + back_rows + hub_back
    ).astype(jnp.bfloat16)
    return (activations, grad_features, grad_w_self, grad_w_neigh, grad_bias)


def solution(mesh):
    in_specs = (
        P(("prow", "pcol"), None),
        P("prow", "pcol", None, None, None),
        P("prow", "pcol", None),
        P("prow", "pcol", None),
        P("prow", "pcol"),
        P("prow", "pcol", None),
        P(("prow", "pcol"), None),
        P(),
        P(),
        P(),
        P(("prow", "pcol"), None),
    )
    out_specs = (P(("prow", "pcol"), None), P(("prow", "pcol"), None), P(), P(), P())
    return jax.shard_map(
        per_device, mesh=mesh, in_specs=in_specs, out_specs=out_specs, check_vma=False
    )
```

```python
import math

import jax
import jax.numpy as jnp
from jax import lax
from jax.sharding import PartitionSpec as P


def _pairwise_allreduce(flat, axes):
    steps = []
    for axis in axes:
        size = lax.axis_size(axis)
        bit = 1
        while bit < size:
            steps.append((axis, size, bit))
            bit *= 2
    x = flat
    for axis, size, bit in steps:
        upper = (lax.axis_index(axis) // bit) % 2 == 1
        half = x.shape[0] // 2
        low, high = x[:half], x[half:]
        keep = jnp.where(upper, high, low)
        send = jnp.where(upper, low, high)
        perm = [(k, k ^ bit) for k in range(size)]
        x = keep + lax.ppermute(send, axis, perm)
    for axis, size, bit in reversed(steps):
        upper = (lax.axis_index(axis) // bit) % 2 == 1
        perm = [(k, k ^ bit) for k in range(size)]
        other = lax.ppermute(x, axis, perm)
        x = jnp.where(upper, jnp.concatenate([other, x]), jnp.concatenate([x, other]))
    return x


def per_device(
    features,
    tile_values,
    tile_rows,
    tile_cols,
    tile_count,
    hub_local,
    hub_edges,
    w_self,
    w_neigh,
    bias,
    cotangent,
):
    vertex_count, feat_width = features.shape
    tile_edge = tile_values.shape[-1]
    slot_count = tile_values.shape[2]
    hub_count = hub_local.shape[-1]
    prow_size = lax.axis_size("prow")
    pcol_size = lax.axis_size("pcol")
    row_tiles = pcol_size * vertex_count // tile_edge
    col_tiles = prow_size * vertex_count // tile_edge
    positions = row_tiles * col_tiles

    tiles = tile_values.reshape(slot_count, tile_edge, tile_edge)
    live = jnp.arange(slot_count, dtype=jnp.int32) < tile_count.reshape(())
    pos = tile_rows.reshape(slot_count) * col_tiles + tile_cols.reshape(slot_count)
    place = (pos[:, None] == jnp.arange(positions, dtype=jnp.int32)[None, :]) & live[:, None]
    dense = jnp.einsum(
        "sp,sab->pab", place.astype(jnp.bfloat16), tiles, preferred_element_type=jnp.bfloat16
    )
    adj = (
        dense.reshape(row_tiles, col_tiles, tile_edge, tile_edge)
        .transpose(0, 2, 1, 3)
        .reshape(row_tiles * tile_edge, col_tiles * tile_edge)
    )

    source_cols = lax.all_gather(features, "prow", axis=0, tiled=True)
    hub_ids = hub_local.reshape(hub_count)
    hub_rows = jnp.take(features, hub_ids, axis=0)
    device_count = prow_size * pcol_size
    hub_features = lax.all_to_all(
        jnp.broadcast_to(hub_rows[None], (device_count, hub_count, feat_width)),
        ("prow", "pcol"),
        0,
        0,
        tiled=True,
    ).reshape(device_count * hub_count, feat_width)

    edges_by_col = hub_edges.reshape(vertex_count, prow_size, pcol_size, hub_count).transpose(
        2, 0, 1, 3
    )
    hub_cols = lax.all_to_all(edges_by_col, "pcol", 0, 0, tiled=True).reshape(
        pcol_size * vertex_count, prow_size * hub_count
    )

    hub_cols, hub_features, source_cols = lax.optimization_barrier(
        (hub_cols, hub_features, source_cols)
    )
    row_sums = jnp.dot(adj, source_cols, preferred_element_type=jnp.float32)
    row_deg = jnp.sum(adj, axis=1, dtype=jnp.float32)
    deg_row = jnp.pad(
        row_deg.reshape(pcol_size, 1, vertex_count), ((0, 0), (0, 0), (0, feat_width - vertex_count))
    )
    packed = jnp.concatenate(
        [row_sums.reshape(pcol_size, vertex_count, feat_width), deg_row], axis=1
    )
    reduced = lax.psum_scatter(
        packed.astype(jnp.bfloat16), "pcol", scatter_dimension=0, tiled=True
    ).astype(jnp.float32)
    own_sums = reduced[0, :vertex_count]
    own_deg = reduced[0, vertex_count, :vertex_count]

    hub_sum = jnp.dot(hub_edges, hub_features, preferred_element_type=jnp.float32)
    degree = own_deg + jnp.sum(hub_edges, axis=1, dtype=jnp.float32)
    aggregate = ((own_sums + hub_sum) / degree[:, None]).astype(jnp.bfloat16)
    pre = (
        jnp.dot(features, w_self, preferred_element_type=jnp.float32)
        + jnp.dot(aggregate, w_neigh, preferred_element_type=jnp.float32)
        + bias[None, :]
    )
    sigma = jax.nn.sigmoid(pre)
    activations = (pre * sigma).astype(jnp.bfloat16)
    dpre = cotangent.astype(jnp.float32) * sigma * (1.0 + pre * (1.0 - sigma))
    dpre_b = dpre.astype(jnp.bfloat16)
    total_rows = prow_size * pcol_size * vertex_count
    factor = 1.0 / math.sqrt(total_rows)
    dagg = jnp.dot(dpre_b, w_neigh.T, preferred_element_type=jnp.float32)
    scaled = (dagg / degree[:, None]).astype(jnp.bfloat16)
    scaled, dpre, dpre_b, aggregate = lax.optimization_barrier((scaled, dpre, dpre_b, aggregate))
    self_part = jnp.dot(features.T, dpre_b, preferred_element_type=jnp.float32)
    neigh_part = jnp.dot(aggregate.T, dpre_b, preferred_element_type=jnp.float32)
    bias_part = jnp.sum(dpre, axis=0)
    grad_pack = jnp.concatenate(
        [
            self_part,
            neigh_part,
            jnp.broadcast_to(bias_part[None, :], (8, feat_width)),
        ],
        axis=0,
    )
    grad_total = _pairwise_allreduce(grad_pack.reshape(-1), ("prow", "pcol")).reshape(
        grad_pack.shape
    )
    grad_w_self = grad_total[:feat_width] * factor
    grad_w_neigh = grad_total[feat_width : 2 * feat_width] * factor
    grad_bias = grad_total[2 * feat_width] * factor

    target_rows = lax.all_gather(scaled, "pcol", axis=0, tiled=True)
    back = lax.dot_general(
        adj, target_rows, (((0,), (0,)), ((), ())), preferred_element_type=jnp.float32
    )

    hub_col_sum = lax.dot_general(
        hub_cols, target_rows, (((0,), (0,)), ((), ())), preferred_element_type=jnp.float32
    )
    back_ext = jnp.concatenate(
        [
            back.reshape(prow_size, vertex_count, feat_width),
            hub_col_sum.reshape(prow_size, hub_count, feat_width),
        ],
        axis=1,
    ).astype(jnp.bfloat16)
    back_own = lax.psum_scatter(back_ext, "prow", scatter_dimension=0, tiled=True)
    back_rows = back_own[0, :vertex_count].astype(jnp.float32)
    own_hubs = back_own[0, vertex_count:]
    one_hot = (jnp.arange(vertex_count, dtype=jnp.int32)[:, None] == hub_ids[None, :]).astype(
        jnp.bfloat16
    )
    hub_back = jnp.dot(one_hot, own_hubs, preferred_element_type=jnp.float32)
    grad_features = (
        jnp.dot(dpre_b, w_self.T, preferred_element_type=jnp.float32) + back_rows + hub_back
    ).astype(jnp.bfloat16)
    return (activations, grad_features, grad_w_self, grad_w_neigh, grad_bias)


def solution(mesh):
    in_specs = (
        P(("prow", "pcol"), None),
        P("prow", "pcol", None, None, None),
        P("prow", "pcol", None),
        P("prow", "pcol", None),
        P("prow", "pcol"),
        P("prow", "pcol", None),
        P(("prow", "pcol"), None),
        P(),
        P(),
        P(),
        P(("prow", "pcol"), None),
    )
    out_specs = (P(("prow", "pcol"), None), P(("prow", "pcol"), None), P(), P(), P())
    return jax.shard_map(
        per_device, mesh=mesh, in_specs=in_specs, out_specs=out_specs, check_vma=False
    )
```

```python
import math

import jax
import jax.numpy as jnp
from jax import lax
from jax.sharding import PartitionSpec as P


def _pairwise_allreduce(flat, axes):
    steps = []
    for axis in axes:
        size = lax.axis_size(axis)
        bit = 1
        while bit < size:
            steps.append((axis, size, bit))
            bit *= 2
    x = flat
    for axis, size, bit in steps:
        upper = (lax.axis_index(axis) // bit) % 2 == 1
        half = x.shape[0] // 2
        low, high = x[:half], x[half:]
        keep = jnp.where(upper, high, low)
        send = jnp.where(upper, low, high)
        perm = [(k, k ^ bit) for k in range(size)]
        x = keep + lax.ppermute(send, axis, perm)
    for axis, size, bit in reversed(steps):
        upper = (lax.axis_index(axis) // bit) % 2 == 1
        perm = [(k, k ^ bit) for k in range(size)]
        other = lax.ppermute(x, axis, perm)
        x = jnp.where(upper, jnp.concatenate([other, x]), jnp.concatenate([x, other]))
    return x


def _pairwise_reduce_scatter(chunks, axis):
    size = lax.axis_size(axis)
    bits = size.bit_length() - 1
    rest = chunks.shape[1:]
    x = (
        chunks.reshape((2,) * bits + rest)
        .transpose(tuple(reversed(range(bits))) + tuple(range(bits, bits + len(rest))))
        .reshape(chunks.shape)
    )
    index = lax.axis_index(axis)
    bit = 1
    while bit < size:
        upper = (index // bit) % 2 == 1
        half = x.shape[0] // 2
        low, high = x[:half], x[half:]
        keep = jnp.where(upper, high, low)
        send = jnp.where(upper, low, high)
        perm = [(k, k ^ bit) for k in range(size)]
        got = lax.ppermute(send, axis, perm)
        x = (keep.astype(jnp.float32) + got.astype(jnp.float32)).astype(chunks.dtype)
        bit *= 2
    return x[0]


def per_device(
    features,
    tile_values,
    tile_rows,
    tile_cols,
    tile_count,
    hub_local,
    hub_edges,
    w_self,
    w_neigh,
    bias,
    cotangent,
):
    vertex_count, feat_width = features.shape
    tile_edge = tile_values.shape[-1]
    slot_count = tile_values.shape[2]
    hub_count = hub_local.shape[-1]
    prow_size = lax.axis_size("prow")
    pcol_size = lax.axis_size("pcol")
    row_tiles = pcol_size * vertex_count // tile_edge
    col_tiles = prow_size * vertex_count // tile_edge
    positions = row_tiles * col_tiles

    tiles = tile_values.reshape(slot_count, tile_edge, tile_edge)
    live = jnp.arange(slot_count, dtype=jnp.int32) < tile_count.reshape(())
    pos = tile_rows.reshape(slot_count) * col_tiles + tile_cols.reshape(slot_count)
    place = (pos[:, None] == jnp.arange(positions, dtype=jnp.int32)[None, :]) & live[:, None]
    dense = jnp.einsum(
        "sp,sab->pab", place.astype(jnp.bfloat16), tiles, preferred_element_type=jnp.bfloat16
    )
    adj = (
        dense.reshape(row_tiles, col_tiles, tile_edge, tile_edge)
        .transpose(0, 2, 1, 3)
        .reshape(row_tiles * tile_edge, col_tiles * tile_edge)
    )

    hub_ids = hub_local.reshape(hub_count)
    hub_rows = jnp.take(features, hub_ids, axis=0)
    payload = jnp.concatenate([features, hub_rows], axis=0)
    gathered = lax.all_gather(payload, "prow", axis=0, tiled=False)
    source_cols = gathered[:, :vertex_count].reshape(prow_size * vertex_count, feat_width)
    hub_col = gathered[:, vertex_count:]
    hub_all = lax.all_gather(
        hub_col.reshape(prow_size * hub_count, feat_width), "pcol", axis=0, tiled=True
    )
    hub_features = (
        hub_all.reshape(pcol_size, prow_size, hub_count, feat_width)
        .transpose(1, 0, 2, 3)
        .reshape(prow_size * pcol_size * hub_count, feat_width)
    )

    edges_by_col = hub_edges.reshape(vertex_count, prow_size, pcol_size, hub_count).transpose(
        2, 0, 1, 3
    )
    hub_cols = lax.all_to_all(edges_by_col, "pcol", 0, 0, tiled=True).reshape(
        pcol_size * vertex_count, prow_size * hub_count
    )

    row_sums = jnp.dot(adj, source_cols, preferred_element_type=jnp.float32)
    row_deg = jnp.sum(adj, axis=1, dtype=jnp.float32)
    split = feat_width // 2
    sums_blocks = row_sums.reshape(pcol_size, vertex_count, feat_width)
    deg_row = jnp.pad(
        row_deg.reshape(pcol_size, 1, vertex_count), ((0, 0), (0, 0), (0, split - vertex_count))
    )
    packed = jnp.concatenate([sums_blocks[:, :, :split], deg_row], axis=1)
    reduced = lax.psum_scatter(
        packed.astype(jnp.bfloat16), "pcol", scatter_dimension=0, tiled=True
    ).astype(jnp.float32)
    other_half = _pairwise_reduce_scatter(
        sums_blocks[:, :, split:].astype(jnp.bfloat16), "pcol"
    ).astype(jnp.float32)
    own_sums = jnp.concatenate([reduced[0, :vertex_count], other_half], axis=1)
    own_deg = reduced[0, vertex_count, :vertex_count]

    hub_sum = jnp.dot(hub_edges, hub_features, preferred_element_type=jnp.float32)
    degree = own_deg + jnp.sum(hub_edges, axis=1, dtype=jnp.float32)
    aggregate = ((own_sums + hub_sum) / degree[:, None]).astype(jnp.bfloat16)
    pre = (
        jnp.dot(features, w_self, preferred_element_type=jnp.float32)
        + jnp.dot(aggregate, w_neigh, preferred_element_type=jnp.float32)
        + bias[None, :]
    )
    sigma = jax.nn.sigmoid(pre)
    activations = (pre * sigma).astype(jnp.bfloat16)
    dpre = cotangent.astype(jnp.float32) * sigma * (1.0 + pre * (1.0 - sigma))
    dpre_b = dpre.astype(jnp.bfloat16)
    total_rows = prow_size * pcol_size * vertex_count
    factor = 1.0 / math.sqrt(total_rows)
    dagg = jnp.dot(dpre_b, w_neigh.T, preferred_element_type=jnp.float32)
    scaled = (dagg / degree[:, None]).astype(jnp.bfloat16)
    scaled, dpre, dpre_b, aggregate = lax.optimization_barrier((scaled, dpre, dpre_b, aggregate))
    self_part = jnp.dot(features.T, dpre_b, preferred_element_type=jnp.float32)
    neigh_part = jnp.dot(aggregate.T, dpre_b, preferred_element_type=jnp.float32)
    bias_part = jnp.sum(dpre, axis=0)
    grad_pack = jnp.concatenate(
        [
            self_part,
            neigh_part,
            jnp.broadcast_to(bias_part[None, :], (8, feat_width)),
        ],
        axis=0,
    )
    grad_total = _pairwise_allreduce(grad_pack.reshape(-1), ("prow", "pcol")).reshape(
        grad_pack.shape
    )
    grad_w_self = grad_total[:feat_width] * factor
    grad_w_neigh = grad_total[feat_width : 2 * feat_width] * factor
    grad_bias = grad_total[2 * feat_width] * factor

    target_rows = lax.all_gather(scaled, "pcol", axis=0, tiled=True)
    back = lax.dot_general(
        adj, target_rows, (((0,), (0,)), ((), ())), preferred_element_type=jnp.float32
    )

    hub_col_sum = lax.dot_general(
        hub_cols, target_rows, (((0,), (0,)), ((), ())), preferred_element_type=jnp.float32
    )
    back_ext = jnp.concatenate(
        [
            back.reshape(prow_size, vertex_count, feat_width),
            hub_col_sum.reshape(prow_size, hub_count, feat_width),
        ],
        axis=1,
    ).astype(jnp.bfloat16)
    back_own = lax.psum_scatter(back_ext, "prow", scatter_dimension=0, tiled=True)
    back_rows = back_own[0, :vertex_count].astype(jnp.float32)
    own_hubs = back_own[0, vertex_count:]
    one_hot = (jnp.arange(vertex_count, dtype=jnp.int32)[:, None] == hub_ids[None, :]).astype(
        jnp.bfloat16
    )
    hub_back = jnp.dot(one_hot, own_hubs, preferred_element_type=jnp.float32)
    grad_features = (
        jnp.dot(dpre_b, w_self.T, preferred_element_type=jnp.float32) + back_rows + hub_back
    ).astype(jnp.bfloat16)
    return (activations, grad_features, grad_w_self, grad_w_neigh, grad_bias)


def solution(mesh):
    in_specs = (
        P(("prow", "pcol"), None),
        P("prow", "pcol", None, None, None),
        P("prow", "pcol", None),
        P("prow", "pcol", None),
        P("prow", "pcol"),
        P("prow", "pcol", None),
        P(("prow", "pcol"), None),
        P(),
        P(),
        P(),
        P(("prow", "pcol"), None),
    )
    out_specs = (P(("prow", "pcol"), None), P(("prow", "pcol"), None), P(), P(), P())
    return jax.shard_map(
        per_device, mesh=mesh, in_specs=in_specs, out_specs=out_specs, check_vma=False
    )
```

```python
import math

import jax
import jax.numpy as jnp
from jax import lax
from jax.sharding import PartitionSpec as P


def _pairwise_allreduce(flat, axes):
    steps = []
    for axis in axes:
        size = lax.axis_size(axis)
        bit = 1
        while bit < size:
            steps.append((axis, size, bit))
            bit *= 2
    x = flat
    for axis, size, bit in steps:
        upper = (lax.axis_index(axis) // bit) % 2 == 1
        half = x.shape[0] // 2
        low, high = x[:half], x[half:]
        keep = jnp.where(upper, high, low)
        send = jnp.where(upper, low, high)
        perm = [(k, k ^ bit) for k in range(size)]
        x = keep + lax.ppermute(send, axis, perm)
    for axis, size, bit in reversed(steps):
        upper = (lax.axis_index(axis) // bit) % 2 == 1
        perm = [(k, k ^ bit) for k in range(size)]
        other = lax.ppermute(x, axis, perm)
        x = jnp.where(upper, jnp.concatenate([other, x]), jnp.concatenate([x, other]))
    return x


def _pairwise_reduce_scatter(chunks, axis):
    size = lax.axis_size(axis)
    bits = size.bit_length() - 1
    rest = chunks.shape[1:]
    x = (
        chunks.reshape((2,) * bits + rest)
        .transpose(tuple(reversed(range(bits))) + tuple(range(bits, bits + len(rest))))
        .reshape(chunks.shape)
    )
    index = lax.axis_index(axis)
    bit = 1
    while bit < size:
        upper = (index // bit) % 2 == 1
        half = x.shape[0] // 2
        low, high = x[:half], x[half:]
        keep = jnp.where(upper, high, low)
        send = jnp.where(upper, low, high)
        perm = [(k, k ^ bit) for k in range(size)]
        got = lax.ppermute(send, axis, perm)
        x = (keep.astype(jnp.float32) + got.astype(jnp.float32)).astype(chunks.dtype)
        bit *= 2
    return x[0]


def per_device(
    features,
    tile_values,
    tile_rows,
    tile_cols,
    tile_count,
    hub_local,
    hub_edges,
    w_self,
    w_neigh,
    bias,
    cotangent,
):
    vertex_count, feat_width = features.shape
    tile_edge = tile_values.shape[-1]
    slot_count = tile_values.shape[2]
    hub_count = hub_local.shape[-1]
    prow_size = lax.axis_size("prow")
    pcol_size = lax.axis_size("pcol")
    row_tiles = pcol_size * vertex_count // tile_edge
    col_tiles = prow_size * vertex_count // tile_edge
    positions = row_tiles * col_tiles

    tiles = tile_values.reshape(slot_count, tile_edge, tile_edge)
    live = jnp.arange(slot_count, dtype=jnp.int32) < tile_count.reshape(())
    pos = tile_rows.reshape(slot_count) * col_tiles + tile_cols.reshape(slot_count)
    place = (pos[:, None] == jnp.arange(positions, dtype=jnp.int32)[None, :]) & live[:, None]
    dense = jnp.einsum(
        "sp,sab->pab", place.astype(jnp.bfloat16), tiles, preferred_element_type=jnp.bfloat16
    )
    adj = (
        dense.reshape(row_tiles, col_tiles, tile_edge, tile_edge)
        .transpose(0, 2, 1, 3)
        .reshape(row_tiles * tile_edge, col_tiles * tile_edge)
    )

    hub_ids = hub_local.reshape(hub_count)
    hub_rows = jnp.take(features, hub_ids, axis=0)
    payload = jnp.concatenate([features, hub_rows], axis=0)
    gathered = lax.all_gather(payload, "prow", axis=0, tiled=False)
    source_cols = gathered[:, :vertex_count].reshape(prow_size * vertex_count, feat_width)
    hub_col = gathered[:, vertex_count:]
    hub_all = lax.all_gather(
        hub_col.reshape(prow_size * hub_count, feat_width), "pcol", axis=0, tiled=True
    )
    hub_features = (
        hub_all.reshape(pcol_size, prow_size, hub_count, feat_width)
        .transpose(1, 0, 2, 3)
        .reshape(prow_size * pcol_size * hub_count, feat_width)
    )

    edges_by_col = hub_edges.reshape(vertex_count, prow_size, pcol_size, hub_count).transpose(
        2, 0, 1, 3
    )
    hub_cols = lax.all_to_all(edges_by_col, "pcol", 0, 0, tiled=True).reshape(
        pcol_size * vertex_count, prow_size * hub_count
    )

    row_sums = jnp.dot(adj, source_cols, preferred_element_type=jnp.float32)
    row_deg = jnp.sum(adj, axis=1, dtype=jnp.float32)
    deg_row = jnp.pad(
        row_deg.reshape(pcol_size, 1, vertex_count),
        ((0, 0), (0, 0), (0, feat_width - vertex_count)),
    )
    packed = jnp.concatenate(
        [row_sums.reshape(pcol_size, vertex_count, feat_width), deg_row], axis=1
    )
    reduced = _pairwise_reduce_scatter(packed.astype(jnp.bfloat16), "pcol").astype(jnp.float32)
    own_sums = reduced[:vertex_count]
    own_deg = reduced[vertex_count, :vertex_count]

    hub_sum = jnp.dot(hub_edges, hub_features, preferred_element_type=jnp.float32)
    degree = own_deg + jnp.sum(hub_edges, axis=1, dtype=jnp.float32)
    aggregate = ((own_sums + hub_sum) / degree[:, None]).astype(jnp.bfloat16)
    pre = (
        jnp.dot(features, w_self, preferred_element_type=jnp.float32)
        + jnp.dot(aggregate, w_neigh, preferred_element_type=jnp.float32)
        + bias[None, :]
    )
    sigma = jax.nn.sigmoid(pre)
    activations = (pre * sigma).astype(jnp.bfloat16)
    dpre = cotangent.astype(jnp.float32) * sigma * (1.0 + pre * (1.0 - sigma))
    dpre_b = dpre.astype(jnp.bfloat16)
    total_rows = prow_size * pcol_size * vertex_count
    factor = 1.0 / math.sqrt(total_rows)
    dagg = jnp.dot(dpre_b, w_neigh.T, preferred_element_type=jnp.float32)
    scaled = (dagg / degree[:, None]).astype(jnp.bfloat16)
    scaled, dpre, dpre_b, aggregate = lax.optimization_barrier((scaled, dpre, dpre_b, aggregate))
    self_part = jnp.dot(features.T, dpre_b, preferred_element_type=jnp.float32)
    neigh_part = jnp.dot(aggregate.T, dpre_b, preferred_element_type=jnp.float32)
    bias_part = jnp.sum(dpre, axis=0)
    grad_pack = jnp.concatenate(
        [
            self_part,
            neigh_part,
            jnp.broadcast_to(bias_part[None, :], (8, feat_width)),
        ],
        axis=0,
    )
    grad_total = _pairwise_allreduce(grad_pack.reshape(-1), ("prow", "pcol")).reshape(
        grad_pack.shape
    )
    grad_w_self = grad_total[:feat_width] * factor
    grad_w_neigh = grad_total[feat_width : 2 * feat_width] * factor
    grad_bias = grad_total[2 * feat_width] * factor

    target_rows = lax.all_gather(scaled, "pcol", axis=0, tiled=True)
    back = lax.dot_general(
        adj, target_rows, (((0,), (0,)), ((), ())), preferred_element_type=jnp.float32
    )

    hub_col_sum = lax.dot_general(
        hub_cols, target_rows, (((0,), (0,)), ((), ())), preferred_element_type=jnp.float32
    )
    back_ext = jnp.concatenate(
        [
            back.reshape(prow_size, vertex_count, feat_width),
            hub_col_sum.reshape(prow_size, hub_count, feat_width),
        ],
        axis=1,
    ).astype(jnp.bfloat16)
    back_own = lax.psum_scatter(back_ext, "prow", scatter_dimension=0, tiled=True)
    back_rows = back_own[0, :vertex_count].astype(jnp.float32)
    own_hubs = back_own[0, vertex_count:]
    one_hot = (jnp.arange(vertex_count, dtype=jnp.int32)[:, None] == hub_ids[None, :]).astype(
        jnp.bfloat16
    )
    hub_back = jnp.dot(one_hot, own_hubs, preferred_element_type=jnp.float32)
    grad_features = (
        jnp.dot(dpre_b, w_self.T, preferred_element_type=jnp.float32) + back_rows + hub_back
    ).astype(jnp.bfloat16)
    return (activations, grad_features, grad_w_self, grad_w_neigh, grad_bias)


def solution(mesh):
    in_specs = (
        P(("prow", "pcol"), None),
        P("prow", "pcol", None, None, None),
        P("prow", "pcol", None),
        P("prow", "pcol", None),
        P("prow", "pcol"),
        P("prow", "pcol", None),
        P(("prow", "pcol"), None),
        P(),
        P(),
        P(),
        P(("prow", "pcol"), None),
    )
    out_specs = (P(("prow", "pcol"), None), P(("prow", "pcol"), None), P(), P(), P())
    return jax.shard_map(
        per_device, mesh=mesh, in_specs=in_specs, out_specs=out_specs, check_vma=False
    )
```

```python
import math

import jax
import jax.numpy as jnp
from jax import lax
from jax.sharding import PartitionSpec as P


def _pairwise_allreduce(flat, axes):
    steps = []
    for axis in axes:
        size = lax.axis_size(axis)
        bit = 1
        while bit < size:
            steps.append((axis, size, bit))
            bit *= 2
    x = flat
    for axis, size, bit in steps:
        upper = (lax.axis_index(axis) // bit) % 2 == 1
        half = x.shape[0] // 2
        low, high = x[:half], x[half:]
        keep = jnp.where(upper, high, low)
        send = jnp.where(upper, low, high)
        perm = [(k, k ^ bit) for k in range(size)]
        x = keep + lax.ppermute(send, axis, perm)
    for axis, size, bit in reversed(steps):
        upper = (lax.axis_index(axis) // bit) % 2 == 1
        perm = [(k, k ^ bit) for k in range(size)]
        other = lax.ppermute(x, axis, perm)
        x = jnp.where(upper, jnp.concatenate([other, x]), jnp.concatenate([x, other]))
    return x


def _pairwise_reduce_scatter(chunks, axis):
    size = lax.axis_size(axis)
    bits = size.bit_length() - 1
    rest = chunks.shape[1:]
    x = (
        chunks.reshape((2,) * bits + rest)
        .transpose(tuple(reversed(range(bits))) + tuple(range(bits, bits + len(rest))))
        .reshape(chunks.shape)
    )
    index = lax.axis_index(axis)
    bit = 1
    while bit < size:
        upper = (index // bit) % 2 == 1
        half = x.shape[0] // 2
        low, high = x[:half], x[half:]
        keep = jnp.where(upper, high, low)
        send = jnp.where(upper, low, high)
        perm = [(k, k ^ bit) for k in range(size)]
        got = lax.ppermute(send, axis, perm)
        x = (keep.astype(jnp.float32) + got.astype(jnp.float32)).astype(chunks.dtype)
        bit *= 2
    return x[0]


def per_device(
    features,
    tile_values,
    tile_rows,
    tile_cols,
    tile_count,
    hub_local,
    hub_edges,
    w_self,
    w_neigh,
    bias,
    cotangent,
):
    vertex_count, feat_width = features.shape
    tile_edge = tile_values.shape[-1]
    slot_count = tile_values.shape[2]
    hub_count = hub_local.shape[-1]
    prow_size = lax.axis_size("prow")
    pcol_size = lax.axis_size("pcol")
    row_tiles = pcol_size * vertex_count // tile_edge
    col_tiles = prow_size * vertex_count // tile_edge
    positions = row_tiles * col_tiles

    tiles = tile_values.reshape(slot_count, tile_edge, tile_edge)
    live = jnp.arange(slot_count, dtype=jnp.int32) < tile_count.reshape(())
    pos = tile_rows.reshape(slot_count) * col_tiles + tile_cols.reshape(slot_count)
    place = (pos[:, None] == jnp.arange(positions, dtype=jnp.int32)[None, :]) & live[:, None]
    dense = jnp.einsum(
        "sp,sab->pab", place.astype(jnp.bfloat16), tiles, preferred_element_type=jnp.bfloat16
    )
    adj = (
        dense.reshape(row_tiles, col_tiles, tile_edge, tile_edge)
        .transpose(0, 2, 1, 3)
        .reshape(row_tiles * tile_edge, col_tiles * tile_edge)
    )

    hub_ids = hub_local.reshape(hub_count)
    hub_rows = jnp.take(features, hub_ids, axis=0)
    payload = jnp.concatenate([features, hub_rows], axis=0)
    gathered = lax.all_gather(payload, "prow", axis=0, tiled=False)
    source_cols = gathered[:, :vertex_count].reshape(prow_size * vertex_count, feat_width)
    hub_col = gathered[:, vertex_count:]
    hub_all = lax.all_gather(
        hub_col.reshape(prow_size * hub_count, feat_width), "pcol", axis=0, tiled=True
    )
    hub_features = (
        hub_all.reshape(pcol_size, prow_size, hub_count, feat_width)
        .transpose(1, 0, 2, 3)
        .reshape(prow_size * pcol_size * hub_count, feat_width)
    )

    edges_by_col = hub_edges.reshape(vertex_count, prow_size, pcol_size, hub_count).transpose(
        2, 0, 1, 3
    )
    hub_cols = lax.all_to_all(edges_by_col, "pcol", 0, 0, tiled=True).reshape(
        pcol_size * vertex_count, prow_size * hub_count
    )

    row_sums = jnp.dot(adj, source_cols, preferred_element_type=jnp.float32)
    row_deg = jnp.sum(adj, axis=1, dtype=jnp.float32)
    split = feat_width // 2
    sums_blocks = row_sums.reshape(pcol_size, vertex_count, feat_width)
    deg_row = jnp.pad(
        row_deg.reshape(pcol_size, 1, vertex_count), ((0, 0), (0, 0), (0, split - vertex_count))
    )
    packed = jnp.concatenate([sums_blocks[:, :, :split], deg_row], axis=1)
    reduced = lax.psum_scatter(
        packed.astype(jnp.bfloat16), "pcol", scatter_dimension=0, tiled=True
    ).astype(jnp.float32)
    other_half = _pairwise_reduce_scatter(
        sums_blocks[:, :, split:].astype(jnp.bfloat16), "pcol"
    ).astype(jnp.float32)
    own_sums = jnp.concatenate([reduced[0, :vertex_count], other_half], axis=1)
    own_deg = reduced[0, vertex_count, :vertex_count]

    hub_sum = jnp.dot(hub_edges, hub_features, preferred_element_type=jnp.float32)
    degree = own_deg + jnp.sum(hub_edges, axis=1, dtype=jnp.float32)
    aggregate = ((own_sums + hub_sum) / degree[:, None]).astype(jnp.bfloat16)
    pre = (
        jnp.dot(features, w_self, preferred_element_type=jnp.float32)
        + jnp.dot(aggregate, w_neigh, preferred_element_type=jnp.float32)
        + bias[None, :]
    )
    sigma = jax.nn.sigmoid(pre)
    activations = (pre * sigma).astype(jnp.bfloat16)
    dpre = cotangent.astype(jnp.float32) * sigma * (1.0 + pre * (1.0 - sigma))
    dpre_b = dpre.astype(jnp.bfloat16)
    total_rows = prow_size * pcol_size * vertex_count
    factor = 1.0 / math.sqrt(total_rows)
    dagg = jnp.dot(dpre_b, w_neigh.T, preferred_element_type=jnp.float32)
    scaled = (dagg / degree[:, None]).astype(jnp.bfloat16)
    scaled, dpre, dpre_b, aggregate = lax.optimization_barrier((scaled, dpre, dpre_b, aggregate))
    self_part = jnp.dot(features.T, dpre_b, preferred_element_type=jnp.float32)
    neigh_part = jnp.dot(aggregate.T, dpre_b, preferred_element_type=jnp.float32)
    bias_part = jnp.sum(dpre, axis=0)
    grad_pack = jnp.concatenate(
        [
            self_part,
            neigh_part,
            jnp.broadcast_to(bias_part[None, :], (8, feat_width)),
        ],
        axis=0,
    )
    grad_total = _pairwise_allreduce(grad_pack.reshape(-1), ("prow", "pcol")).reshape(
        grad_pack.shape
    )
    grad_w_self = grad_total[:feat_width] * factor
    grad_w_neigh = grad_total[feat_width : 2 * feat_width] * factor
    grad_bias = grad_total[2 * feat_width] * factor

    target_rows = lax.all_gather(scaled, "pcol", axis=0, tiled=True)
    back = lax.dot_general(
        adj, target_rows, (((0,), (0,)), ((), ())), preferred_element_type=jnp.float32
    )

    hub_col_sum = lax.dot_general(
        hub_cols, target_rows, (((0,), (0,)), ((), ())), preferred_element_type=jnp.float32
    )
    back_ext = jnp.concatenate(
        [
            back.reshape(prow_size, vertex_count, feat_width),
            hub_col_sum.reshape(prow_size, hub_count, feat_width),
        ],
        axis=1,
    ).astype(jnp.bfloat16)
    back_own = _pairwise_reduce_scatter(back_ext, "prow")
    back_rows = back_own[:vertex_count].astype(jnp.float32)
    own_hubs = back_own[vertex_count:]
    one_hot = (jnp.arange(vertex_count, dtype=jnp.int32)[:, None] == hub_ids[None, :]).astype(
        jnp.bfloat16
    )
    hub_back = jnp.dot(one_hot, own_hubs, preferred_element_type=jnp.float32)
    grad_features = (
        jnp.dot(dpre_b, w_self.T, preferred_element_type=jnp.float32) + back_rows + hub_back
    ).astype(jnp.bfloat16)
    return (activations, grad_features, grad_w_self, grad_w_neigh, grad_bias)


def solution(mesh):
    in_specs = (
        P(("prow", "pcol"), None),
        P("prow", "pcol", None, None, None),
        P("prow", "pcol", None),
        P("prow", "pcol", None),
        P("prow", "pcol"),
        P("prow", "pcol", None),
        P(("prow", "pcol"), None),
        P(),
        P(),
        P(),
        P(("prow", "pcol"), None),
    )
    out_specs = (P(("prow", "pcol"), None), P(("prow", "pcol"), None), P(), P(), P())
    return jax.shard_map(
        per_device, mesh=mesh, in_specs=in_specs, out_specs=out_specs, check_vma=False
    )
```

```python
import math

import jax
import jax.numpy as jnp
from jax import lax
from jax.sharding import PartitionSpec as P


def _pairwise_allreduce(flat, axes):
    steps = []
    for axis in axes:
        size = lax.axis_size(axis)
        bit = 1
        while bit < size:
            steps.append((axis, size, bit))
            bit *= 2
    x = flat
    for axis, size, bit in steps:
        upper = (lax.axis_index(axis) // bit) % 2 == 1
        half = x.shape[0] // 2
        low, high = x[:half], x[half:]
        keep = jnp.where(upper, high, low)
        send = jnp.where(upper, low, high)
        perm = [(k, k ^ bit) for k in range(size)]
        x = keep + lax.ppermute(send, axis, perm)
    for axis, size, bit in reversed(steps):
        upper = (lax.axis_index(axis) // bit) % 2 == 1
        perm = [(k, k ^ bit) for k in range(size)]
        other = lax.ppermute(x, axis, perm)
        x = jnp.where(upper, jnp.concatenate([other, x]), jnp.concatenate([x, other]))
    return x


def _pairwise_reduce_scatter(chunks, axis):
    size = lax.axis_size(axis)
    bits = size.bit_length() - 1
    rest = chunks.shape[1:]
    x = (
        chunks.reshape((2,) * bits + rest)
        .transpose(tuple(reversed(range(bits))) + tuple(range(bits, bits + len(rest))))
        .reshape(chunks.shape)
    )
    index = lax.axis_index(axis)
    bit = 1
    while bit < size:
        upper = (index // bit) % 2 == 1
        half = x.shape[0] // 2
        low, high = x[:half], x[half:]
        keep = jnp.where(upper, high, low)
        send = jnp.where(upper, low, high)
        perm = [(k, k ^ bit) for k in range(size)]
        got = lax.ppermute(send, axis, perm)
        x = (keep.astype(jnp.float32) + got.astype(jnp.float32)).astype(chunks.dtype)
        bit *= 2
    return x[0]


def per_device(
    features,
    tile_values,
    tile_rows,
    tile_cols,
    tile_count,
    hub_local,
    hub_edges,
    w_self,
    w_neigh,
    bias,
    cotangent,
):
    vertex_count, feat_width = features.shape
    tile_edge = tile_values.shape[-1]
    slot_count = tile_values.shape[2]
    hub_count = hub_local.shape[-1]
    prow_size = lax.axis_size("prow")
    pcol_size = lax.axis_size("pcol")
    row_tiles = pcol_size * vertex_count // tile_edge
    col_tiles = prow_size * vertex_count // tile_edge
    positions = row_tiles * col_tiles

    tiles = tile_values.reshape(slot_count, tile_edge, tile_edge)
    live = jnp.arange(slot_count, dtype=jnp.int32) < tile_count.reshape(())
    pos = tile_rows.reshape(slot_count) * col_tiles + tile_cols.reshape(slot_count)
    place = (pos[:, None] == jnp.arange(positions, dtype=jnp.int32)[None, :]) & live[:, None]
    dense = jnp.einsum(
        "sp,sab->pab", place.astype(jnp.bfloat16), tiles, preferred_element_type=jnp.bfloat16
    )
    adj = (
        dense.reshape(row_tiles, col_tiles, tile_edge, tile_edge)
        .transpose(0, 2, 1, 3)
        .reshape(row_tiles * tile_edge, col_tiles * tile_edge)
    )

    hub_ids = hub_local.reshape(hub_count)
    hub_rows = jnp.take(features, hub_ids, axis=0)
    payload = jnp.concatenate([features, hub_rows], axis=0)
    gathered = lax.all_gather(payload, "prow", axis=0, tiled=False)
    source_cols = gathered[:, :vertex_count].reshape(prow_size * vertex_count, feat_width)
    hub_col = gathered[:, vertex_count:].reshape(prow_size * hub_count, feat_width)

    edges_by_col = hub_edges.reshape(vertex_count, prow_size, pcol_size, hub_count).transpose(
        2, 0, 1, 3
    )
    hub_cols = lax.all_to_all(edges_by_col, "pcol", 0, 0, tiled=True).reshape(
        pcol_size * vertex_count, prow_size * hub_count
    )

    row_sums = jnp.dot(adj, source_cols, preferred_element_type=jnp.float32) + jnp.dot(
        hub_cols, hub_col, preferred_element_type=jnp.float32
    )
    row_deg = jnp.sum(adj, axis=1, dtype=jnp.float32)
    split = feat_width // 2
    sums_blocks = row_sums.reshape(pcol_size, vertex_count, feat_width)
    deg_row = jnp.pad(
        row_deg.reshape(pcol_size, 1, vertex_count), ((0, 0), (0, 0), (0, split - vertex_count))
    )
    packed = jnp.concatenate([sums_blocks[:, :, :split], deg_row], axis=1)
    reduced = lax.psum_scatter(
        packed.astype(jnp.bfloat16), "pcol", scatter_dimension=0, tiled=True
    ).astype(jnp.float32)
    other_half = _pairwise_reduce_scatter(
        sums_blocks[:, :, split:].astype(jnp.bfloat16), "pcol"
    ).astype(jnp.float32)
    own_sums = jnp.concatenate([reduced[0, :vertex_count], other_half], axis=1)
    own_deg = reduced[0, vertex_count, :vertex_count]

    degree = own_deg + jnp.sum(hub_edges, axis=1, dtype=jnp.float32)
    aggregate = (own_sums / degree[:, None]).astype(jnp.bfloat16)
    pre = (
        jnp.dot(features, w_self, preferred_element_type=jnp.float32)
        + jnp.dot(aggregate, w_neigh, preferred_element_type=jnp.float32)
        + bias[None, :]
    )
    sigma = jax.nn.sigmoid(pre)
    activations = (pre * sigma).astype(jnp.bfloat16)
    dpre = cotangent.astype(jnp.float32) * sigma * (1.0 + pre * (1.0 - sigma))
    dpre_b = dpre.astype(jnp.bfloat16)
    total_rows = prow_size * pcol_size * vertex_count
    factor = 1.0 / math.sqrt(total_rows)
    dagg = jnp.dot(dpre_b, w_neigh.T, preferred_element_type=jnp.float32)
    scaled = (dagg / degree[:, None]).astype(jnp.bfloat16)
    scaled, dpre, dpre_b, aggregate = lax.optimization_barrier((scaled, dpre, dpre_b, aggregate))
    self_part = jnp.dot(features.T, dpre_b, preferred_element_type=jnp.float32)
    neigh_part = jnp.dot(aggregate.T, dpre_b, preferred_element_type=jnp.float32)
    bias_part = jnp.sum(dpre, axis=0)
    grad_pack = jnp.concatenate(
        [
            self_part,
            neigh_part,
            jnp.broadcast_to(bias_part[None, :], (8, feat_width)),
        ],
        axis=0,
    )
    grad_total = _pairwise_allreduce(grad_pack.reshape(-1), ("prow", "pcol")).reshape(
        grad_pack.shape
    )
    grad_w_self = grad_total[:feat_width] * factor
    grad_w_neigh = grad_total[feat_width : 2 * feat_width] * factor
    grad_bias = grad_total[2 * feat_width] * factor

    target_rows = lax.all_gather(scaled, "pcol", axis=0, tiled=True)
    back = lax.dot_general(
        adj, target_rows, (((0,), (0,)), ((), ())), preferred_element_type=jnp.float32
    )

    hub_col_sum = lax.dot_general(
        hub_cols, target_rows, (((0,), (0,)), ((), ())), preferred_element_type=jnp.float32
    )
    back_ext = jnp.concatenate(
        [
            back.reshape(prow_size, vertex_count, feat_width),
            hub_col_sum.reshape(prow_size, hub_count, feat_width),
        ],
        axis=1,
    ).astype(jnp.bfloat16)
    back_own = _pairwise_reduce_scatter(back_ext, "prow")
    back_rows = back_own[:vertex_count].astype(jnp.float32)
    own_hubs = back_own[vertex_count:]
    one_hot = (jnp.arange(vertex_count, dtype=jnp.int32)[:, None] == hub_ids[None, :]).astype(
        jnp.bfloat16
    )
    hub_back = jnp.dot(one_hot, own_hubs, preferred_element_type=jnp.float32)
    grad_features = (
        jnp.dot(dpre_b, w_self.T, preferred_element_type=jnp.float32) + back_rows + hub_back
    ).astype(jnp.bfloat16)
    return (activations, grad_features, grad_w_self, grad_w_neigh, grad_bias)


def solution(mesh):
    in_specs = (
        P(("prow", "pcol"), None),
        P("prow", "pcol", None, None, None),
        P("prow", "pcol", None),
        P("prow", "pcol", None),
        P("prow", "pcol"),
        P("prow", "pcol", None),
        P(("prow", "pcol"), None),
        P(),
        P(),
        P(),
        P(("prow", "pcol"), None),
    )
    out_specs = (P(("prow", "pcol"), None), P(("prow", "pcol"), None), P(), P(), P())
    return jax.shard_map(
        per_device, mesh=mesh, in_specs=in_specs, out_specs=out_specs, check_vma=False
    )
```

```python
import math

import jax
import jax.numpy as jnp
from jax import lax
from jax.sharding import PartitionSpec as P


def _pairwise_allreduce(flat, axes):
    steps = []
    for axis in axes:
        size = lax.axis_size(axis)
        bit = 1
        while bit < size:
            steps.append((axis, size, bit))
            bit *= 2
    x = flat
    for axis, size, bit in steps:
        upper = (lax.axis_index(axis) // bit) % 2 == 1
        half = x.shape[0] // 2
        low, high = x[:half], x[half:]
        keep = jnp.where(upper, high, low)
        send = jnp.where(upper, low, high)
        perm = [(k, k ^ bit) for k in range(size)]
        x = keep + lax.ppermute(send, axis, perm)
    for axis, size, bit in reversed(steps):
        upper = (lax.axis_index(axis) // bit) % 2 == 1
        perm = [(k, k ^ bit) for k in range(size)]
        other = lax.ppermute(x, axis, perm)
        x = jnp.where(upper, jnp.concatenate([other, x]), jnp.concatenate([x, other]))
    return x


def _pairwise_reduce_scatter(chunks, axis, order=None):
    size = lax.axis_size(axis)
    bits = size.bit_length() - 1
    if order is None:
        order = [1 << k for k in range(bits)]
    place = [
        sum(((idx // b) % 2) << (bits - 1 - k) for k, b in enumerate(order))
        for idx in range(size)
    ]
    source = [0] * size
    for idx, p in enumerate(place):
        source[p] = idx
    x = jnp.concatenate([chunks[idx : idx + 1] for idx in source], axis=0)
    index = lax.axis_index(axis)
    for bit in order:
        upper = (index // bit) % 2 == 1
        half = x.shape[0] // 2
        low, high = x[:half], x[half:]
        keep = jnp.where(upper, high, low)
        send = jnp.where(upper, low, high)
        perm = [(k, k ^ bit) for k in range(size)]
        got = lax.ppermute(send, axis, perm)
        x = (keep.astype(jnp.float32) + got.astype(jnp.float32)).astype(chunks.dtype)
    return x[0]


def per_device(
    features,
    tile_values,
    tile_rows,
    tile_cols,
    tile_count,
    hub_local,
    hub_edges,
    w_self,
    w_neigh,
    bias,
    cotangent,
):
    vertex_count, feat_width = features.shape
    tile_edge = tile_values.shape[-1]
    slot_count = tile_values.shape[2]
    hub_count = hub_local.shape[-1]
    prow_size = lax.axis_size("prow")
    pcol_size = lax.axis_size("pcol")
    row_tiles = pcol_size * vertex_count // tile_edge
    col_tiles = prow_size * vertex_count // tile_edge
    positions = row_tiles * col_tiles

    tiles = tile_values.reshape(slot_count, tile_edge, tile_edge)
    live = jnp.arange(slot_count, dtype=jnp.int32) < tile_count.reshape(())
    pos = tile_rows.reshape(slot_count) * col_tiles + tile_cols.reshape(slot_count)
    place = (pos[:, None] == jnp.arange(positions, dtype=jnp.int32)[None, :]) & live[:, None]
    dense = jnp.einsum(
        "sp,sab->pab", place.astype(jnp.bfloat16), tiles, preferred_element_type=jnp.bfloat16
    )
    adj = (
        dense.reshape(row_tiles, col_tiles, tile_edge, tile_edge)
        .transpose(0, 2, 1, 3)
        .reshape(row_tiles * tile_edge, col_tiles * tile_edge)
    )

    hub_ids = hub_local.reshape(hub_count)
    hub_rows = jnp.take(features, hub_ids, axis=0)
    payload = jnp.concatenate([features, hub_rows], axis=0)
    gathered = lax.all_gather(payload, "prow", axis=0, tiled=False)
    source_cols = gathered[:, :vertex_count].reshape(prow_size * vertex_count, feat_width)
    hub_col = gathered[:, vertex_count:].reshape(prow_size * hub_count, feat_width)

    edges_by_col = hub_edges.reshape(vertex_count, prow_size, pcol_size, hub_count).transpose(
        2, 0, 1, 3
    )
    hub_cols = lax.all_to_all(edges_by_col, "pcol", 0, 0, tiled=True).reshape(
        pcol_size * vertex_count, prow_size * hub_count
    )

    row_sums = jnp.dot(adj, source_cols, preferred_element_type=jnp.float32) + jnp.dot(
        hub_cols, hub_col, preferred_element_type=jnp.float32
    )
    row_deg = jnp.sum(adj, axis=1, dtype=jnp.float32)
    split = feat_width // 2
    sums_blocks = row_sums.reshape(pcol_size, vertex_count, feat_width).astype(jnp.bfloat16)
    deg_row = jnp.pad(
        row_deg.reshape(pcol_size, 1, vertex_count), ((0, 0), (0, 0), (0, split - vertex_count))
    ).astype(jnp.bfloat16)
    first = jnp.concatenate([sums_blocks[:, :, :split], deg_row], axis=1)
    pcol_bits = [1 << k for k in range(pcol_size.bit_length() - 1)]
    reduced = _pairwise_reduce_scatter(first, "pcol", pcol_bits).astype(jnp.float32)
    other_order = pcol_bits[1:2] + pcol_bits[:1] + pcol_bits[2:]
    other_half = _pairwise_reduce_scatter(
        sums_blocks[:, :, split:], "pcol", other_order
    ).astype(jnp.float32)
    own_sums = jnp.concatenate([reduced[:vertex_count], other_half], axis=1)
    own_deg = reduced[vertex_count, :vertex_count]

    degree = own_deg + jnp.sum(hub_edges, axis=1, dtype=jnp.float32)
    aggregate = (own_sums / degree[:, None]).astype(jnp.bfloat16)
    pre = (
        jnp.dot(features, w_self, preferred_element_type=jnp.float32)
        + jnp.dot(aggregate, w_neigh, preferred_element_type=jnp.float32)
        + bias[None, :]
    )
    sigma = jax.nn.sigmoid(pre)
    activations = (pre * sigma).astype(jnp.bfloat16)
    dpre = cotangent.astype(jnp.float32) * sigma * (1.0 + pre * (1.0 - sigma))
    dpre_b = dpre.astype(jnp.bfloat16)
    total_rows = prow_size * pcol_size * vertex_count
    factor = 1.0 / math.sqrt(total_rows)
    dagg = jnp.dot(dpre_b, w_neigh.T, preferred_element_type=jnp.float32)
    scaled = (dagg / degree[:, None]).astype(jnp.bfloat16)
    scaled, dpre, dpre_b, aggregate = lax.optimization_barrier((scaled, dpre, dpre_b, aggregate))
    self_part = jnp.dot(features.T, dpre_b, preferred_element_type=jnp.float32)
    neigh_part = jnp.dot(aggregate.T, dpre_b, preferred_element_type=jnp.float32)
    bias_part = jnp.sum(dpre, axis=0)
    grad_pack = jnp.concatenate(
        [
            self_part,
            neigh_part,
            jnp.broadcast_to(bias_part[None, :], (8, feat_width)),
        ],
        axis=0,
    )
    grad_total = _pairwise_allreduce(grad_pack.reshape(-1), ("prow", "pcol")).reshape(
        grad_pack.shape
    )
    grad_w_self = grad_total[:feat_width] * factor
    grad_w_neigh = grad_total[feat_width : 2 * feat_width] * factor
    grad_bias = grad_total[2 * feat_width] * factor

    target_rows = lax.all_gather(scaled, "pcol", axis=0, tiled=True)
    back = lax.dot_general(
        adj, target_rows, (((0,), (0,)), ((), ())), preferred_element_type=jnp.float32
    )

    hub_col_sum = lax.dot_general(
        hub_cols, target_rows, (((0,), (0,)), ((), ())), preferred_element_type=jnp.float32
    )
    back_ext = jnp.concatenate(
        [
            back.reshape(prow_size, vertex_count, feat_width),
            hub_col_sum.reshape(prow_size, hub_count, feat_width),
        ],
        axis=1,
    ).astype(jnp.bfloat16)
    back_own = _pairwise_reduce_scatter(back_ext, "prow")
    back_rows = back_own[:vertex_count].astype(jnp.float32)
    own_hubs = back_own[vertex_count:]
    one_hot = (jnp.arange(vertex_count, dtype=jnp.int32)[:, None] == hub_ids[None, :]).astype(
        jnp.bfloat16
    )
    hub_back = jnp.dot(one_hot, own_hubs, preferred_element_type=jnp.float32)
    grad_features = (
        jnp.dot(dpre_b, w_self.T, preferred_element_type=jnp.float32) + back_rows + hub_back
    ).astype(jnp.bfloat16)
    return (activations, grad_features, grad_w_self, grad_w_neigh, grad_bias)


def solution(mesh):
    in_specs = (
        P(("prow", "pcol"), None),
        P("prow", "pcol", None, None, None),
        P("prow", "pcol", None),
        P("prow", "pcol", None),
        P("prow", "pcol"),
        P("prow", "pcol", None),
        P(("prow", "pcol"), None),
        P(),
        P(),
        P(),
        P(("prow", "pcol"), None),
    )
    out_specs = (P(("prow", "pcol"), None), P(("prow", "pcol"), None), P(), P(), P())
    return jax.shard_map(
        per_device, mesh=mesh, in_specs=in_specs, out_specs=out_specs, check_vma=False
    )
```

```python
import math

import jax
import jax.numpy as jnp
from jax import lax
from jax.sharding import PartitionSpec as P


def _pairwise_allreduce(flat, axes):
    steps = []
    for axis in axes:
        size = lax.axis_size(axis)
        bit = 1
        while bit < size:
            steps.append((axis, size, bit))
            bit *= 2
    x = flat
    for axis, size, bit in steps:
        upper = (lax.axis_index(axis) // bit) % 2 == 1
        half = x.shape[0] // 2
        low, high = x[:half], x[half:]
        keep = jnp.where(upper, high, low)
        send = jnp.where(upper, low, high)
        perm = [(k, k ^ bit) for k in range(size)]
        x = keep + lax.ppermute(send, axis, perm)
    for axis, size, bit in reversed(steps):
        upper = (lax.axis_index(axis) // bit) % 2 == 1
        perm = [(k, k ^ bit) for k in range(size)]
        other = lax.ppermute(x, axis, perm)
        x = jnp.where(upper, jnp.concatenate([other, x]), jnp.concatenate([x, other]))
    return x


def _pairwise_reduce_scatter(chunks, axis, order=None):
    size = lax.axis_size(axis)
    bits = size.bit_length() - 1
    if order is None:
        order = [1 << k for k in range(bits)]
    place = [
        sum(((idx // b) % 2) << (bits - 1 - k) for k, b in enumerate(order))
        for idx in range(size)
    ]
    source = [0] * size
    for idx, p in enumerate(place):
        source[p] = idx
    x = jnp.concatenate([chunks[idx : idx + 1] for idx in source], axis=0)
    index = lax.axis_index(axis)
    for bit in order:
        upper = (index // bit) % 2 == 1
        half = x.shape[0] // 2
        low, high = x[:half], x[half:]
        keep = jnp.where(upper, high, low)
        send = jnp.where(upper, low, high)
        perm = [(k, k ^ bit) for k in range(size)]
        got = lax.ppermute(send, axis, perm)
        x = (keep.astype(jnp.float32) + got.astype(jnp.float32)).astype(chunks.dtype)
    return x[0]


def _pairwise_all_gather(chunk, axis, order):
    size = lax.axis_size(axis)
    index = lax.axis_index(axis)
    x = chunk[None]
    for bit in order:
        upper = (index // bit) % 2 == 1
        perm = [(k, k ^ bit) for k in range(size)]
        other = lax.ppermute(x, axis, perm)
        x = jnp.where(upper, jnp.concatenate([other, x]), jnp.concatenate([x, other]))
    place = [
        sum(((idx // b) % 2) << k for k, b in enumerate(order)) for idx in range(size)
    ]
    return jnp.concatenate([x[p : p + 1] for p in place], axis=0)


def per_device(
    features,
    tile_values,
    tile_rows,
    tile_cols,
    tile_count,
    hub_local,
    hub_edges,
    w_self,
    w_neigh,
    bias,
    cotangent,
):
    vertex_count, feat_width = features.shape
    tile_edge = tile_values.shape[-1]
    slot_count = tile_values.shape[2]
    hub_count = hub_local.shape[-1]
    prow_size = lax.axis_size("prow")
    pcol_size = lax.axis_size("pcol")
    row_tiles = pcol_size * vertex_count // tile_edge
    col_tiles = prow_size * vertex_count // tile_edge
    positions = row_tiles * col_tiles

    tiles = tile_values.reshape(slot_count, tile_edge, tile_edge)
    live = jnp.arange(slot_count, dtype=jnp.int32) < tile_count.reshape(())
    pos = tile_rows.reshape(slot_count) * col_tiles + tile_cols.reshape(slot_count)
    place = (pos[:, None] == jnp.arange(positions, dtype=jnp.int32)[None, :]) & live[:, None]
    dense = jnp.einsum(
        "sp,sab->pab", place.astype(jnp.bfloat16), tiles, preferred_element_type=jnp.bfloat16
    )
    adj = (
        dense.reshape(row_tiles, col_tiles, tile_edge, tile_edge)
        .transpose(0, 2, 1, 3)
        .reshape(row_tiles * tile_edge, col_tiles * tile_edge)
    )

    hub_ids = hub_local.reshape(hub_count)
    hub_rows = jnp.take(features, hub_ids, axis=0)
    payload = jnp.concatenate([features, hub_rows], axis=0)
    gathered = lax.all_gather(payload, "prow", axis=0, tiled=False)
    source_cols = gathered[:, :vertex_count].reshape(prow_size * vertex_count, feat_width)
    hub_col = gathered[:, vertex_count:].reshape(prow_size * hub_count, feat_width)

    edges_by_col = hub_edges.reshape(vertex_count, prow_size, pcol_size, hub_count).transpose(
        2, 0, 1, 3
    )
    hub_cols = lax.all_to_all(edges_by_col, "pcol", 0, 0, tiled=True).reshape(
        pcol_size * vertex_count, prow_size * hub_count
    )

    row_sums = jnp.dot(adj, source_cols, preferred_element_type=jnp.float32) + jnp.dot(
        hub_cols, hub_col, preferred_element_type=jnp.float32
    )
    row_deg = jnp.sum(adj, axis=1, dtype=jnp.float32)
    split = feat_width // 2
    sums_blocks = row_sums.reshape(pcol_size, vertex_count, feat_width).astype(jnp.bfloat16)
    deg_row = jnp.pad(
        row_deg.reshape(pcol_size, 1, vertex_count), ((0, 0), (0, 0), (0, split - vertex_count))
    ).astype(jnp.bfloat16)
    first = jnp.concatenate([sums_blocks[:, :, :split], deg_row], axis=1)
    pcol_bits = [1 << k for k in range(pcol_size.bit_length() - 1)]
    reduced = _pairwise_reduce_scatter(first, "pcol", pcol_bits).astype(jnp.float32)
    other_order = pcol_bits[1:2] + pcol_bits[:1] + pcol_bits[2:]
    other_half = _pairwise_reduce_scatter(
        sums_blocks[:, :, split:], "pcol", other_order
    ).astype(jnp.float32)
    own_sums = jnp.concatenate([reduced[:vertex_count], other_half], axis=1)
    own_deg = reduced[vertex_count, :vertex_count]

    degree = own_deg + jnp.sum(hub_edges, axis=1, dtype=jnp.float32)
    aggregate = (own_sums / degree[:, None]).astype(jnp.bfloat16)
    pre = (
        jnp.dot(features, w_self, preferred_element_type=jnp.float32)
        + jnp.dot(aggregate, w_neigh, preferred_element_type=jnp.float32)
        + bias[None, :]
    )
    sigma = jax.nn.sigmoid(pre)
    activations = (pre * sigma).astype(jnp.bfloat16)
    dpre = cotangent.astype(jnp.float32) * sigma * (1.0 + pre * (1.0 - sigma))
    dpre_b = dpre.astype(jnp.bfloat16)
    total_rows = prow_size * pcol_size * vertex_count
    factor = 1.0 / math.sqrt(total_rows)
    dagg = jnp.dot(dpre_b, w_neigh.T, preferred_element_type=jnp.float32)
    scaled = (dagg / degree[:, None]).astype(jnp.bfloat16)
    scaled, dpre, dpre_b, aggregate = lax.optimization_barrier((scaled, dpre, dpre_b, aggregate))
    self_part = jnp.dot(features.T, dpre_b, preferred_element_type=jnp.float32)
    neigh_part = jnp.dot(aggregate.T, dpre_b, preferred_element_type=jnp.float32)
    bias_part = jnp.sum(dpre, axis=0)
    grad_pack = jnp.concatenate(
        [
            self_part,
            neigh_part,
            jnp.broadcast_to(bias_part[None, :], (8, feat_width)),
        ],
        axis=0,
    )
    grad_total = _pairwise_allreduce(grad_pack.reshape(-1), ("prow", "pcol")).reshape(
        grad_pack.shape
    )
    grad_w_self = grad_total[:feat_width] * factor
    grad_w_neigh = grad_total[feat_width : 2 * feat_width] * factor
    grad_bias = grad_total[2 * feat_width] * factor

    pcol_bits = [1 << k for k in range(pcol_size.bit_length() - 1)]
    half_cols = feat_width // 2
    gather_a = _pairwise_all_gather(scaled[:, :half_cols], "pcol", pcol_bits[::-1])
    gather_b = _pairwise_all_gather(
        scaled[:, half_cols:], "pcol", pcol_bits[2:][::-1] + pcol_bits[:2]
    )
    target_rows = jnp.concatenate([gather_a, gather_b], axis=2).reshape(
        pcol_size * vertex_count, feat_width
    )
    back = lax.dot_general(
        adj, target_rows, (((0,), (0,)), ((), ())), preferred_element_type=jnp.float32
    )

    hub_col_sum = lax.dot_general(
        hub_cols, target_rows, (((0,), (0,)), ((), ())), preferred_element_type=jnp.float32
    )
    back_ext = jnp.concatenate(
        [
            back.reshape(prow_size, vertex_count, feat_width),
            hub_col_sum.reshape(prow_size, hub_count, feat_width),
        ],
        axis=1,
    ).astype(jnp.bfloat16)
    back_own = _pairwise_reduce_scatter(back_ext, "prow")
    back_rows = back_own[:vertex_count].astype(jnp.float32)
    own_hubs = back_own[vertex_count:]
    one_hot = (jnp.arange(vertex_count, dtype=jnp.int32)[:, None] == hub_ids[None, :]).astype(
        jnp.bfloat16
    )
    hub_back = jnp.dot(one_hot, own_hubs, preferred_element_type=jnp.float32)
    grad_features = (
        jnp.dot(dpre_b, w_self.T, preferred_element_type=jnp.float32) + back_rows + hub_back
    ).astype(jnp.bfloat16)
    return (activations, grad_features, grad_w_self, grad_w_neigh, grad_bias)


def solution(mesh):
    in_specs = (
        P(("prow", "pcol"), None),
        P("prow", "pcol", None, None, None),
        P("prow", "pcol", None),
        P("prow", "pcol", None),
        P("prow", "pcol"),
        P("prow", "pcol", None),
        P(("prow", "pcol"), None),
        P(),
        P(),
        P(),
        P(("prow", "pcol"), None),
    )
    out_specs = (P(("prow", "pcol"), None), P(("prow", "pcol"), None), P(), P(), P())
    return jax.shard_map(
        per_device, mesh=mesh, in_specs=in_specs, out_specs=out_specs, check_vma=False
    )
```

```python
import math

import jax
import jax.numpy as jnp
from jax import lax
from jax.sharding import PartitionSpec as P


def _pairwise_allreduce(flat, axes):
    steps = []
    for axis in axes:
        size = lax.axis_size(axis)
        bit = 1
        while bit < size:
            steps.append((axis, size, bit))
            bit *= 2
    x = flat
    for axis, size, bit in steps:
        upper = (lax.axis_index(axis) // bit) % 2 == 1
        half = x.shape[0] // 2
        low, high = x[:half], x[half:]
        keep = jnp.where(upper, high, low)
        send = jnp.where(upper, low, high)
        perm = [(k, k ^ bit) for k in range(size)]
        x = keep + lax.ppermute(send, axis, perm)
    for axis, size, bit in reversed(steps):
        upper = (lax.axis_index(axis) // bit) % 2 == 1
        perm = [(k, k ^ bit) for k in range(size)]
        other = lax.ppermute(x, axis, perm)
        x = jnp.where(upper, jnp.concatenate([other, x]), jnp.concatenate([x, other]))
    return x


def _pairwise_reduce_scatter(chunks, axis, order=None):
    size = lax.axis_size(axis)
    bits = size.bit_length() - 1
    if order is None:
        order = [1 << k for k in range(bits)]
    place = [
        sum(((idx // b) % 2) << (bits - 1 - k) for k, b in enumerate(order))
        for idx in range(size)
    ]
    source = [0] * size
    for idx, p in enumerate(place):
        source[p] = idx
    x = jnp.concatenate([chunks[idx : idx + 1] for idx in source], axis=0)
    index = lax.axis_index(axis)
    for bit in order:
        upper = (index // bit) % 2 == 1
        half = x.shape[0] // 2
        low, high = x[:half], x[half:]
        keep = jnp.where(upper, high, low)
        send = jnp.where(upper, low, high)
        perm = [(k, k ^ bit) for k in range(size)]
        got = lax.ppermute(send, axis, perm)
        x = (keep.astype(jnp.float32) + got.astype(jnp.float32)).astype(chunks.dtype)
    return x[0]


def _pairwise_all_gather(chunk, axis, order):
    size = lax.axis_size(axis)
    index = lax.axis_index(axis)
    x = chunk[None]
    for bit in order:
        upper = (index // bit) % 2 == 1
        perm = [(k, k ^ bit) for k in range(size)]
        other = lax.ppermute(x, axis, perm)
        x = jnp.where(upper, jnp.concatenate([other, x]), jnp.concatenate([x, other]))
    place = [
        sum(((idx // b) % 2) << k for k, b in enumerate(order)) for idx in range(size)
    ]
    return jnp.concatenate([x[p : p + 1] for p in place], axis=0)


def per_device(
    features,
    tile_values,
    tile_rows,
    tile_cols,
    tile_count,
    hub_local,
    hub_edges,
    w_self,
    w_neigh,
    bias,
    cotangent,
):
    vertex_count, feat_width = features.shape
    tile_edge = tile_values.shape[-1]
    slot_count = tile_values.shape[2]
    hub_count = hub_local.shape[-1]
    prow_size = lax.axis_size("prow")
    pcol_size = lax.axis_size("pcol")
    row_tiles = pcol_size * vertex_count // tile_edge
    col_tiles = prow_size * vertex_count // tile_edge
    positions = row_tiles * col_tiles

    tiles = tile_values.reshape(slot_count, tile_edge, tile_edge)
    live = jnp.arange(slot_count, dtype=jnp.int32) < tile_count.reshape(())
    pos = tile_rows.reshape(slot_count) * col_tiles + tile_cols.reshape(slot_count)
    place = (pos[:, None] == jnp.arange(positions, dtype=jnp.int32)[None, :]) & live[:, None]
    dense = jnp.einsum(
        "sp,sab->pab", place.astype(jnp.bfloat16), tiles, preferred_element_type=jnp.bfloat16
    )
    adj = (
        dense.reshape(row_tiles, col_tiles, tile_edge, tile_edge)
        .transpose(0, 2, 1, 3)
        .reshape(row_tiles * tile_edge, col_tiles * tile_edge)
    )

    hub_ids = hub_local.reshape(hub_count)
    hub_rows = jnp.take(features, hub_ids, axis=0)
    payload = jnp.concatenate([features, hub_rows], axis=0)
    gathered = lax.all_gather(payload, "prow", axis=0, tiled=False)
    source_cols = gathered[:, :vertex_count].reshape(prow_size * vertex_count, feat_width)
    hub_col = gathered[:, vertex_count:].reshape(prow_size * hub_count, feat_width)

    edges_by_col = hub_edges.reshape(vertex_count, prow_size, pcol_size, hub_count).transpose(
        2, 0, 1, 3
    )
    hub_cols = lax.all_to_all(edges_by_col, "pcol", 0, 0, tiled=True).reshape(
        pcol_size * vertex_count, prow_size * hub_count
    )

    row_sums = jnp.dot(adj, source_cols, preferred_element_type=jnp.float32) + jnp.dot(
        hub_cols, hub_col, preferred_element_type=jnp.float32
    )
    row_deg = jnp.sum(adj, axis=1, dtype=jnp.float32)
    split = feat_width // 2
    sums_blocks = row_sums.reshape(pcol_size, vertex_count, feat_width).astype(jnp.bfloat16)
    deg_row = jnp.pad(
        row_deg.reshape(pcol_size, 1, vertex_count), ((0, 0), (0, 0), (0, split - vertex_count))
    ).astype(jnp.bfloat16)
    first = jnp.concatenate([sums_blocks[:, :, :split], deg_row], axis=1)
    pcol_bits = [1 << k for k in range(pcol_size.bit_length() - 1)]
    reduced = _pairwise_reduce_scatter(first, "pcol", pcol_bits).astype(jnp.float32)
    other_order = pcol_bits[1:2] + pcol_bits[:1] + pcol_bits[2:]
    other_half = _pairwise_reduce_scatter(
        sums_blocks[:, :, split:], "pcol", other_order
    ).astype(jnp.float32)
    own_sums = jnp.concatenate([reduced[:vertex_count], other_half], axis=1)
    adj_t = adj.T
    hub_cols_t = hub_cols.T
    adj_t, hub_cols_t, own_sums = lax.optimization_barrier((adj_t, hub_cols_t, own_sums))
    own_deg = reduced[vertex_count, :vertex_count]

    degree = own_deg + jnp.sum(hub_edges, axis=1, dtype=jnp.float32)
    aggregate = (own_sums / degree[:, None]).astype(jnp.bfloat16)
    pre = (
        jnp.dot(features, w_self, preferred_element_type=jnp.float32)
        + jnp.dot(aggregate, w_neigh, preferred_element_type=jnp.float32)
        + bias[None, :]
    )
    sigma = jax.nn.sigmoid(pre)
    activations = (pre * sigma).astype(jnp.bfloat16)
    dpre = cotangent.astype(jnp.float32) * sigma * (1.0 + pre * (1.0 - sigma))
    dpre_b = dpre.astype(jnp.bfloat16)
    total_rows = prow_size * pcol_size * vertex_count
    factor = 1.0 / math.sqrt(total_rows)
    dagg = jnp.dot(dpre_b, w_neigh.T, preferred_element_type=jnp.float32)
    scaled = (dagg / degree[:, None]).astype(jnp.bfloat16)
    scaled, dpre, dpre_b, aggregate = lax.optimization_barrier((scaled, dpre, dpre_b, aggregate))
    self_part = jnp.dot(features.T, dpre_b, preferred_element_type=jnp.float32)
    neigh_part = jnp.dot(aggregate.T, dpre_b, preferred_element_type=jnp.float32)
    bias_part = jnp.sum(dpre, axis=0)
    grad_pack = jnp.concatenate(
        [
            self_part,
            neigh_part,
            jnp.broadcast_to(bias_part[None, :], (8, feat_width)),
        ],
        axis=0,
    )

    pcol_bits = [1 << k for k in range(pcol_size.bit_length() - 1)]
    half_cols = feat_width // 2
    gather_a = _pairwise_all_gather(scaled[:, :half_cols], "pcol", pcol_bits[::-1])
    gather_b = _pairwise_all_gather(
        scaled[:, half_cols:], "pcol", pcol_bits[2:][::-1] + pcol_bits[:2]
    )
    target_rows = jnp.concatenate([gather_a, gather_b], axis=2).reshape(
        pcol_size * vertex_count, feat_width
    )
    grad_pack, target_rows = lax.optimization_barrier((grad_pack, target_rows))
    grad_total = _pairwise_allreduce(grad_pack.reshape(-1), ("prow", "pcol")).reshape(
        grad_pack.shape
    )
    grad_w_self = grad_total[:feat_width] * factor
    grad_w_neigh = grad_total[feat_width : 2 * feat_width] * factor
    grad_bias = grad_total[2 * feat_width] * factor
    back = jnp.dot(adj_t, target_rows, preferred_element_type=jnp.float32)

    hub_col_sum = jnp.dot(hub_cols_t, target_rows, preferred_element_type=jnp.float32)
    back_ext = jnp.concatenate(
        [
            back.reshape(prow_size, vertex_count, feat_width),
            hub_col_sum.reshape(prow_size, hub_count, feat_width),
        ],
        axis=1,
    ).astype(jnp.bfloat16)
    back_own = _pairwise_reduce_scatter(back_ext, "prow")
    back_rows = back_own[:vertex_count].astype(jnp.float32)
    own_hubs = back_own[vertex_count:]
    one_hot = (jnp.arange(vertex_count, dtype=jnp.int32)[:, None] == hub_ids[None, :]).astype(
        jnp.bfloat16
    )
    hub_back = jnp.dot(one_hot, own_hubs, preferred_element_type=jnp.float32)
    grad_features = (
        jnp.dot(dpre_b, w_self.T, preferred_element_type=jnp.float32) + back_rows + hub_back
    ).astype(jnp.bfloat16)
    return (activations, grad_features, grad_w_self, grad_w_neigh, grad_bias)


def solution(mesh):
    in_specs = (
        P(("prow", "pcol"), None),
        P("prow", "pcol", None, None, None),
        P("prow", "pcol", None),
        P("prow", "pcol", None),
        P("prow", "pcol"),
        P("prow", "pcol", None),
        P(("prow", "pcol"), None),
        P(),
        P(),
        P(),
        P(("prow", "pcol"), None),
    )
    out_specs = (P(("prow", "pcol"), None), P(("prow", "pcol"), None), P(), P(), P())
    return jax.shard_map(
        per_device, mesh=mesh, in_specs=in_specs, out_specs=out_specs, check_vma=False
    )
```

```python
import math

import jax
import jax.numpy as jnp
from jax import lax
from jax.sharding import PartitionSpec as P


def _pairwise_allreduce(flat, axes, swap=False):
    steps = []
    for axis in axes:
        size = lax.axis_size(axis)
        bits = [1 << k for k in range(size.bit_length() - 1)]
        if swap:
            bits = bits[1:2] + bits[:1] + bits[2:]
        steps.extend((axis, size, bit) for bit in bits)
    x = flat
    for axis, size, bit in steps:
        upper = (lax.axis_index(axis) // bit) % 2 == 1
        half = x.shape[0] // 2
        low, high = x[:half], x[half:]
        keep = jnp.where(upper, high, low)
        send = jnp.where(upper, low, high)
        perm = [(k, k ^ bit) for k in range(size)]
        x = keep + lax.ppermute(send, axis, perm)
    for axis, size, bit in reversed(steps):
        upper = (lax.axis_index(axis) // bit) % 2 == 1
        perm = [(k, k ^ bit) for k in range(size)]
        other = lax.ppermute(x, axis, perm)
        x = jnp.where(upper, jnp.concatenate([other, x]), jnp.concatenate([x, other]))
    return x


def _pairwise_reduce_scatter(chunks, axis, order=None):
    size = lax.axis_size(axis)
    bits = size.bit_length() - 1
    if order is None:
        order = [1 << k for k in range(bits)]
    place = [
        sum(((idx // b) % 2) << (bits - 1 - k) for k, b in enumerate(order))
        for idx in range(size)
    ]
    source = [0] * size
    for idx, p in enumerate(place):
        source[p] = idx
    x = jnp.concatenate([chunks[idx : idx + 1] for idx in source], axis=0)
    index = lax.axis_index(axis)
    for bit in order:
        upper = (index // bit) % 2 == 1
        half = x.shape[0] // 2
        low, high = x[:half], x[half:]
        keep = jnp.where(upper, high, low)
        send = jnp.where(upper, low, high)
        perm = [(k, k ^ bit) for k in range(size)]
        got = lax.ppermute(send, axis, perm)
        x = (keep.astype(jnp.float32) + got.astype(jnp.float32)).astype(chunks.dtype)
    return x[0]


def per_device(
    features,
    tile_values,
    tile_rows,
    tile_cols,
    tile_count,
    hub_local,
    hub_edges,
    w_self,
    w_neigh,
    bias,
    cotangent,
):
    vertex_count, feat_width = features.shape
    tile_edge = tile_values.shape[-1]
    slot_count = tile_values.shape[2]
    hub_count = hub_local.shape[-1]
    prow_size = lax.axis_size("prow")
    pcol_size = lax.axis_size("pcol")
    row_tiles = pcol_size * vertex_count // tile_edge
    col_tiles = prow_size * vertex_count // tile_edge
    positions = row_tiles * col_tiles

    tiles = tile_values.reshape(slot_count, tile_edge, tile_edge)
    live = jnp.arange(slot_count, dtype=jnp.int32) < tile_count.reshape(())
    pos = tile_rows.reshape(slot_count) * col_tiles + tile_cols.reshape(slot_count)
    place = (pos[:, None] == jnp.arange(positions, dtype=jnp.int32)[None, :]) & live[:, None]
    dense = jnp.einsum(
        "sp,sab->pab", place.astype(jnp.bfloat16), tiles, preferred_element_type=jnp.bfloat16
    )
    adj = (
        dense.reshape(row_tiles, col_tiles, tile_edge, tile_edge)
        .transpose(0, 2, 1, 3)
        .reshape(row_tiles * tile_edge, col_tiles * tile_edge)
    )

    hub_ids = hub_local.reshape(hub_count)
    hub_rows = jnp.take(features, hub_ids, axis=0)
    payload = jnp.concatenate([features, hub_rows], axis=0)
    gathered = lax.all_gather(payload, "prow", axis=0, tiled=False)
    source_cols = gathered[:, :vertex_count].reshape(prow_size * vertex_count, feat_width)
    hub_col = gathered[:, vertex_count:].reshape(prow_size * hub_count, feat_width)

    edges_by_col = hub_edges.reshape(vertex_count, prow_size, pcol_size, hub_count).transpose(
        2, 0, 1, 3
    )
    hub_cols = lax.all_to_all(edges_by_col, "pcol", 0, 0, tiled=True).reshape(
        pcol_size * vertex_count, prow_size * hub_count
    )

    row_sums = jnp.dot(adj, source_cols, preferred_element_type=jnp.float32) + jnp.dot(
        hub_cols, hub_col, preferred_element_type=jnp.float32
    )
    row_deg = jnp.sum(adj, axis=1, dtype=jnp.float32)
    split = feat_width // 2
    sums_blocks = row_sums.reshape(pcol_size, vertex_count, feat_width).astype(jnp.bfloat16)
    deg_row = jnp.pad(
        row_deg.reshape(pcol_size, 1, vertex_count), ((0, 0), (0, 0), (0, split - vertex_count))
    ).astype(jnp.bfloat16)
    first = jnp.concatenate([sums_blocks[:, :, :split], deg_row], axis=1)
    pcol_bits = [1 << k for k in range(pcol_size.bit_length() - 1)]
    reduced = _pairwise_reduce_scatter(first, "pcol", pcol_bits).astype(jnp.float32)
    other_order = pcol_bits[1:2] + pcol_bits[:1] + pcol_bits[2:]
    other_half = _pairwise_reduce_scatter(
        sums_blocks[:, :, split:], "pcol", other_order
    ).astype(jnp.float32)
    own_sums = jnp.concatenate([reduced[:vertex_count], other_half], axis=1)
    own_deg = reduced[vertex_count, :vertex_count]

    degree = own_deg + jnp.sum(hub_edges, axis=1, dtype=jnp.float32)
    aggregate = (own_sums / degree[:, None]).astype(jnp.bfloat16)
    pre = (
        jnp.dot(features, w_self, preferred_element_type=jnp.float32)
        + jnp.dot(aggregate, w_neigh, preferred_element_type=jnp.float32)
        + bias[None, :]
    )
    sigma = jax.nn.sigmoid(pre)
    activations = (pre * sigma).astype(jnp.bfloat16)
    dpre = cotangent.astype(jnp.float32) * sigma * (1.0 + pre * (1.0 - sigma))
    dpre_b = dpre.astype(jnp.bfloat16)
    total_rows = prow_size * pcol_size * vertex_count
    factor = 1.0 / math.sqrt(total_rows)
    dagg = jnp.dot(dpre_b, w_neigh.T, preferred_element_type=jnp.float32)
    scaled = (dagg / degree[:, None]).astype(jnp.bfloat16)
    scaled, dpre, dpre_b, aggregate = lax.optimization_barrier((scaled, dpre, dpre_b, aggregate))
    self_part = jnp.dot(features.T, dpre_b, preferred_element_type=jnp.float32)
    neigh_part = jnp.dot(aggregate.T, dpre_b, preferred_element_type=jnp.float32)
    bias_part = jnp.sum(dpre, axis=0)
    grad_pack = jnp.concatenate(
        [
            self_part,
            neigh_part,
            jnp.broadcast_to(bias_part[None, :], (8, feat_width)),
        ],
        axis=0,
    )
    grad_flat = grad_pack.reshape(-1)
    grad_half = grad_flat.shape[0] // 2
    grad_total = jnp.concatenate(
        [
            _pairwise_allreduce(grad_flat[:grad_half], ("prow", "pcol")),
            _pairwise_allreduce(grad_flat[grad_half:], ("prow", "pcol"), swap=True),
        ]
    ).reshape(grad_pack.shape)
    grad_w_self = grad_total[:feat_width] * factor
    grad_w_neigh = grad_total[feat_width : 2 * feat_width] * factor
    grad_bias = grad_total[2 * feat_width] * factor

    target_rows = lax.all_gather(scaled, "pcol", axis=0, tiled=True)
    back = lax.dot_general(
        adj, target_rows, (((0,), (0,)), ((), ())), preferred_element_type=jnp.float32
    )

    hub_col_sum = lax.dot_general(
        hub_cols, target_rows, (((0,), (0,)), ((), ())), preferred_element_type=jnp.float32
    )
    back_ext = jnp.concatenate(
        [
            back.reshape(prow_size, vertex_count, feat_width),
            hub_col_sum.reshape(prow_size, hub_count, feat_width),
        ],
        axis=1,
    ).astype(jnp.bfloat16)
    back_own = _pairwise_reduce_scatter(back_ext, "prow")
    back_rows = back_own[:vertex_count].astype(jnp.float32)
    own_hubs = back_own[vertex_count:]
    one_hot = (jnp.arange(vertex_count, dtype=jnp.int32)[:, None] == hub_ids[None, :]).astype(
        jnp.bfloat16
    )
    hub_back = jnp.dot(one_hot, own_hubs, preferred_element_type=jnp.float32)
    grad_features = (
        jnp.dot(dpre_b, w_self.T, preferred_element_type=jnp.float32) + back_rows + hub_back
    ).astype(jnp.bfloat16)
    return (activations, grad_features, grad_w_self, grad_w_neigh, grad_bias)


def solution(mesh):
    in_specs = (
        P(("prow", "pcol"), None),
        P("prow", "pcol", None, None, None),
        P("prow", "pcol", None),
        P("prow", "pcol", None),
        P("prow", "pcol"),
        P("prow", "pcol", None),
        P(("prow", "pcol"), None),
        P(),
        P(),
        P(),
        P(("prow", "pcol"), None),
    )
    out_specs = (P(("prow", "pcol"), None), P(("prow", "pcol"), None), P(), P(), P())
    return jax.shard_map(
        per_device, mesh=mesh, in_specs=in_specs, out_specs=out_specs, check_vma=False
    )
```

```python
import math

import jax
import jax.numpy as jnp
from jax import lax
from jax.sharding import PartitionSpec as P


def _pairwise_allreduce(flat, axes):
    steps = []
    for axis in axes:
        size = lax.axis_size(axis)
        bit = 1
        while bit < size:
            steps.append((axis, size, bit))
            bit *= 2
    x = flat
    for axis, size, bit in steps:
        upper = (lax.axis_index(axis) // bit) % 2 == 1
        half = x.shape[0] // 2
        low, high = x[:half], x[half:]
        keep = jnp.where(upper, high, low)
        send = jnp.where(upper, low, high)
        perm = [(k, k ^ bit) for k in range(size)]
        x = keep + lax.ppermute(send, axis, perm)
    for axis, size, bit in reversed(steps):
        upper = (lax.axis_index(axis) // bit) % 2 == 1
        perm = [(k, k ^ bit) for k in range(size)]
        other = lax.ppermute(x, axis, perm)
        x = jnp.where(upper, jnp.concatenate([other, x]), jnp.concatenate([x, other]))
    return x


def _pairwise_reduce_scatter(chunks, axis, order=None):
    size = lax.axis_size(axis)
    bits = size.bit_length() - 1
    if order is None:
        order = [1 << k for k in range(bits)]
    place = [
        sum(((idx // b) % 2) << (bits - 1 - k) for k, b in enumerate(order))
        for idx in range(size)
    ]
    source = [0] * size
    for idx, p in enumerate(place):
        source[p] = idx
    x = jnp.concatenate([chunks[idx : idx + 1] for idx in source], axis=0)
    index = lax.axis_index(axis)
    for bit in order:
        upper = (index // bit) % 2 == 1
        half = x.shape[0] // 2
        low, high = x[:half], x[half:]
        keep = jnp.where(upper, high, low)
        send = jnp.where(upper, low, high)
        perm = [(k, k ^ bit) for k in range(size)]
        got = lax.ppermute(send, axis, perm)
        x = (keep.astype(jnp.float32) + got.astype(jnp.float32)).astype(chunks.dtype)
    return x[0]


def per_device(
    features,
    tile_values,
    tile_rows,
    tile_cols,
    tile_count,
    hub_local,
    hub_edges,
    w_self,
    w_neigh,
    bias,
    cotangent,
):
    vertex_count, feat_width = features.shape
    tile_edge = tile_values.shape[-1]
    slot_count = tile_values.shape[2]
    hub_count = hub_local.shape[-1]
    prow_size = lax.axis_size("prow")
    pcol_size = lax.axis_size("pcol")
    row_tiles = pcol_size * vertex_count // tile_edge
    col_tiles = prow_size * vertex_count // tile_edge
    positions = row_tiles * col_tiles

    tiles = tile_values.reshape(slot_count, tile_edge, tile_edge)
    live = jnp.arange(slot_count, dtype=jnp.int32) < tile_count.reshape(())
    pos = tile_rows.reshape(slot_count) * col_tiles + tile_cols.reshape(slot_count)
    place = (pos[:, None] == jnp.arange(positions, dtype=jnp.int32)[None, :]) & live[:, None]
    dense = jnp.einsum(
        "sp,sab->pab", place.astype(jnp.bfloat16), tiles, preferred_element_type=jnp.bfloat16
    )
    adj = (
        dense.reshape(row_tiles, col_tiles, tile_edge, tile_edge)
        .transpose(0, 2, 1, 3)
        .reshape(row_tiles * tile_edge, col_tiles * tile_edge)
    )

    hub_ids = hub_local.reshape(hub_count)
    hub_rows = jnp.take(features, hub_ids, axis=0)
    payload = jnp.concatenate([features, hub_rows], axis=0)
    gathered = lax.all_gather(payload, "prow", axis=0, tiled=False)
    source_cols = gathered[:, :vertex_count].reshape(prow_size * vertex_count, feat_width)
    hub_col = gathered[:, vertex_count:].reshape(prow_size * hub_count, feat_width)

    edges_by_col = (
        hub_edges.T.reshape(prow_size, pcol_size, hub_count, vertex_count)
        .transpose(1, 0, 2, 3)
        .reshape(pcol_size, prow_size * hub_count, vertex_count)
    )
    hub_cols_t = (
        lax.all_to_all(edges_by_col, "pcol", 0, 0, tiled=True)
        .transpose(1, 0, 2)
        .reshape(prow_size * hub_count, pcol_size * vertex_count)
    )

    row_sums = jnp.dot(adj, source_cols, preferred_element_type=jnp.float32) + lax.dot_general(
        hub_cols_t, hub_col, (((0,), (0,)), ((), ())), preferred_element_type=jnp.float32
    )
    row_deg = jnp.sum(adj, axis=1, dtype=jnp.float32)
    split = feat_width // 2
    sums_blocks = row_sums.reshape(pcol_size, vertex_count, feat_width).astype(jnp.bfloat16)
    deg_row = jnp.pad(
        row_deg.reshape(pcol_size, 1, vertex_count), ((0, 0), (0, 0), (0, split - vertex_count))
    ).astype(jnp.bfloat16)
    first = jnp.concatenate([sums_blocks[:, :, :split], deg_row], axis=1)
    pcol_bits = [1 << k for k in range(pcol_size.bit_length() - 1)]
    reduced = _pairwise_reduce_scatter(first, "pcol", pcol_bits).astype(jnp.float32)
    other_order = pcol_bits[1:2] + pcol_bits[:1] + pcol_bits[2:]
    other_half = _pairwise_reduce_scatter(
        sums_blocks[:, :, split:], "pcol", other_order
    ).astype(jnp.float32)
    own_sums = jnp.concatenate([reduced[:vertex_count], other_half], axis=1)
    own_deg = reduced[vertex_count, :vertex_count]

    degree = own_deg + jnp.sum(hub_edges, axis=1, dtype=jnp.float32)
    aggregate = (own_sums / degree[:, None]).astype(jnp.bfloat16)
    pre = (
        jnp.dot(features, w_self, preferred_element_type=jnp.float32)
        + jnp.dot(aggregate, w_neigh, preferred_element_type=jnp.float32)
        + bias[None, :]
    )
    sigma = jax.nn.sigmoid(pre)
    activations = (pre * sigma).astype(jnp.bfloat16)
    dpre = cotangent.astype(jnp.float32) * sigma * (1.0 + pre * (1.0 - sigma))
    dpre_b = dpre.astype(jnp.bfloat16)
    total_rows = prow_size * pcol_size * vertex_count
    factor = 1.0 / math.sqrt(total_rows)
    dagg = jnp.dot(dpre_b, w_neigh.T, preferred_element_type=jnp.float32)
    scaled = (dagg / degree[:, None]).astype(jnp.bfloat16)
    scaled, dpre, dpre_b, aggregate = lax.optimization_barrier((scaled, dpre, dpre_b, aggregate))
    self_part = jnp.dot(features.T, dpre_b, preferred_element_type=jnp.float32)
    neigh_part = jnp.dot(aggregate.T, dpre_b, preferred_element_type=jnp.float32)
    bias_part = jnp.sum(dpre, axis=0)
    grad_pack = jnp.concatenate(
        [
            self_part,
            neigh_part,
            jnp.broadcast_to(bias_part[None, :], (8, feat_width)),
        ],
        axis=0,
    )
    grad_total = _pairwise_allreduce(grad_pack.reshape(-1), ("prow", "pcol")).reshape(
        grad_pack.shape
    )
    grad_w_self = grad_total[:feat_width] * factor
    grad_w_neigh = grad_total[feat_width : 2 * feat_width] * factor
    grad_bias = grad_total[2 * feat_width] * factor

    target_rows = lax.all_gather(scaled, "pcol", axis=0, tiled=True)
    back = lax.dot_general(
        adj, target_rows, (((0,), (0,)), ((), ())), preferred_element_type=jnp.float32
    )

    hub_col_sum = jnp.dot(hub_cols_t, target_rows, preferred_element_type=jnp.float32)
    back_ext = jnp.concatenate(
        [
            back.reshape(prow_size, vertex_count, feat_width),
            hub_col_sum.reshape(prow_size, hub_count, feat_width),
        ],
        axis=1,
    ).astype(jnp.bfloat16)
    back_own = _pairwise_reduce_scatter(back_ext, "prow")
    back_rows = back_own[:vertex_count].astype(jnp.float32)
    own_hubs = back_own[vertex_count:]
    one_hot = (jnp.arange(vertex_count, dtype=jnp.int32)[:, None] == hub_ids[None, :]).astype(
        jnp.bfloat16
    )
    hub_back = jnp.dot(one_hot, own_hubs, preferred_element_type=jnp.float32)
    grad_features = (
        jnp.dot(dpre_b, w_self.T, preferred_element_type=jnp.float32) + back_rows + hub_back
    ).astype(jnp.bfloat16)
    return (activations, grad_features, grad_w_self, grad_w_neigh, grad_bias)


def solution(mesh):
    in_specs = (
        P(("prow", "pcol"), None),
        P("prow", "pcol", None, None, None),
        P("prow", "pcol", None),
        P("prow", "pcol", None),
        P("prow", "pcol"),
        P("prow", "pcol", None),
        P(("prow", "pcol"), None),
        P(),
        P(),
        P(),
        P(("prow", "pcol"), None),
    )
    out_specs = (P(("prow", "pcol"), None), P(("prow", "pcol"), None), P(), P(), P())
    return jax.shard_map(
        per_device, mesh=mesh, in_specs=in_specs, out_specs=out_specs, check_vma=False
    )
```

```python
import math

import jax
import jax.numpy as jnp
from jax import lax
from jax.sharding import PartitionSpec as P


def _pairwise_allreduce(flat, axes):
    steps = []
    for axis in axes:
        size = lax.axis_size(axis)
        bit = 1
        while bit < size:
            steps.append((axis, size, bit))
            bit *= 2
    x = flat
    for axis, size, bit in steps:
        upper = (lax.axis_index(axis) // bit) % 2 == 1
        half = x.shape[0] // 2
        low, high = x[:half], x[half:]
        keep = jnp.where(upper, high, low)
        send = jnp.where(upper, low, high)
        perm = [(k, k ^ bit) for k in range(size)]
        x = keep + lax.ppermute(send, axis, perm)
    for axis, size, bit in reversed(steps):
        upper = (lax.axis_index(axis) // bit) % 2 == 1
        perm = [(k, k ^ bit) for k in range(size)]
        other = lax.ppermute(x, axis, perm)
        x = jnp.where(upper, jnp.concatenate([other, x]), jnp.concatenate([x, other]))
    return x


def _pairwise_reduce_scatter(chunks, axis, order=None):
    size = lax.axis_size(axis)
    bits = size.bit_length() - 1
    if order is None:
        order = [1 << k for k in range(bits)]
    place = [
        sum(((idx // b) % 2) << (bits - 1 - k) for k, b in enumerate(order))
        for idx in range(size)
    ]
    source = [0] * size
    for idx, p in enumerate(place):
        source[p] = idx
    x = jnp.concatenate([chunks[idx : idx + 1] for idx in source], axis=0)
    index = lax.axis_index(axis)
    for bit in order:
        upper = (index // bit) % 2 == 1
        half = x.shape[0] // 2
        low, high = x[:half], x[half:]
        keep = jnp.where(upper, high, low)
        send = jnp.where(upper, low, high)
        perm = [(k, k ^ bit) for k in range(size)]
        got = lax.ppermute(send, axis, perm)
        x = (keep.astype(jnp.float32) + got.astype(jnp.float32)).astype(chunks.dtype)
    return x[0]


def per_device(
    features,
    tile_values,
    tile_rows,
    tile_cols,
    tile_count,
    hub_local,
    hub_edges,
    w_self,
    w_neigh,
    bias,
    cotangent,
):
    vertex_count, feat_width = features.shape
    tile_edge = tile_values.shape[-1]
    slot_count = tile_values.shape[2]
    hub_count = hub_local.shape[-1]
    prow_size = lax.axis_size("prow")
    pcol_size = lax.axis_size("pcol")
    row_tiles = pcol_size * vertex_count // tile_edge
    col_tiles = prow_size * vertex_count // tile_edge
    positions = row_tiles * col_tiles

    tiles = tile_values.reshape(slot_count, tile_edge, tile_edge)
    live = jnp.arange(slot_count, dtype=jnp.int32) < tile_count.reshape(())
    pos = tile_rows.reshape(slot_count) * col_tiles + tile_cols.reshape(slot_count)
    place = (pos[:, None] == jnp.arange(positions, dtype=jnp.int32)[None, :]) & live[:, None]
    dense = jnp.einsum(
        "sp,sab->pab", place.astype(jnp.bfloat16), tiles, preferred_element_type=jnp.bfloat16
    )
    adj = (
        dense.reshape(row_tiles, col_tiles, tile_edge, tile_edge)
        .transpose(0, 2, 1, 3)
        .reshape(row_tiles * tile_edge, col_tiles * tile_edge)
    )

    hub_ids = hub_local.reshape(hub_count)
    hub_rows = jnp.take(features, hub_ids, axis=0)
    payload = jnp.concatenate([features, hub_rows], axis=0)
    gathered = lax.all_gather(payload, "prow", axis=0, tiled=False)
    source_cols = gathered[:, :vertex_count].reshape(prow_size * vertex_count, feat_width)
    hub_col = gathered[:, vertex_count:].reshape(prow_size * hub_count, feat_width)

    edges_by_col = hub_edges.reshape(vertex_count, prow_size, pcol_size, hub_count).transpose(
        2, 0, 1, 3
    )
    hub_cols = lax.all_to_all(edges_by_col, "pcol", 0, 0, tiled=True).reshape(
        pcol_size * vertex_count, prow_size * hub_count
    )

    row_sums = jnp.dot(adj, source_cols, preferred_element_type=jnp.float32) + jnp.dot(
        hub_cols, hub_col, preferred_element_type=jnp.float32
    )
    row_deg = jnp.sum(adj, axis=1, dtype=jnp.float32)
    split = feat_width // 2
    sums_blocks = row_sums.reshape(pcol_size, vertex_count, feat_width).astype(jnp.bfloat16)
    deg_row = jnp.pad(
        row_deg.reshape(pcol_size, 1, vertex_count), ((0, 0), (0, 0), (0, split - vertex_count))
    ).astype(jnp.bfloat16)
    first = jnp.concatenate([sums_blocks[:, :, :split], deg_row], axis=1)
    pcol_bits = [1 << k for k in range(pcol_size.bit_length() - 1)]
    reduced = _pairwise_reduce_scatter(first, "pcol", pcol_bits).astype(jnp.float32)
    other_order = pcol_bits[1:2] + pcol_bits[:1] + pcol_bits[2:]
    other_half = _pairwise_reduce_scatter(
        sums_blocks[:, :, split:], "pcol", other_order
    ).astype(jnp.float32)
    own_sums = jnp.concatenate([reduced[:vertex_count], other_half], axis=1)
    own_deg = reduced[vertex_count, :vertex_count]

    degree = own_deg + jnp.sum(hub_edges, axis=1, dtype=jnp.float32)
    aggregate = (own_sums / degree[:, None]).astype(jnp.bfloat16)
    pre = (
        jnp.dot(features, w_self, preferred_element_type=jnp.float32)
        + jnp.dot(aggregate, w_neigh, preferred_element_type=jnp.float32)
        + bias[None, :]
    )
    sigma = jax.nn.sigmoid(pre)
    activations = (pre * sigma).astype(jnp.bfloat16)
    dpre = cotangent.astype(jnp.float32) * sigma * (1.0 + pre * (1.0 - sigma))
    dpre_b = dpre.astype(jnp.bfloat16)
    total_rows = prow_size * pcol_size * vertex_count
    factor = 1.0 / math.sqrt(total_rows)
    dagg = jnp.dot(dpre_b, w_neigh.T, preferred_element_type=jnp.float32)
    scaled = (dagg / degree[:, None]).astype(jnp.bfloat16)
    scaled, dpre, dpre_b, aggregate = lax.optimization_barrier((scaled, dpre, dpre_b, aggregate))
    self_part = jnp.dot(features.T, dpre_b, preferred_element_type=jnp.float32)
    neigh_part = jnp.dot(aggregate.T, dpre_b, preferred_element_type=jnp.float32)
    bias_part = jnp.sum(dpre, axis=0)
    grad_pack = jnp.concatenate(
        [
            self_part,
            neigh_part,
            jnp.broadcast_to(bias_part[None, :], (8, feat_width)),
        ],
        axis=0,
    )
    grad_total = _pairwise_allreduce(grad_pack.reshape(-1), ("prow", "pcol")).reshape(
        grad_pack.shape
    )
    grad_w_self = grad_total[:feat_width] * factor
    grad_w_neigh = grad_total[feat_width : 2 * feat_width] * factor
    grad_bias = grad_total[2 * feat_width] * factor

    target_rows = lax.all_gather(scaled, "pcol", axis=0, tiled=True)
    back_lhs = jnp.concatenate(
        [
            adj.T.reshape(prow_size, vertex_count, pcol_size * vertex_count),
            hub_cols.T.reshape(prow_size, hub_count, pcol_size * vertex_count),
        ],
        axis=1,
    ).reshape(prow_size * (vertex_count + hub_count), pcol_size * vertex_count)
    back_ext = (
        jnp.dot(back_lhs, target_rows, preferred_element_type=jnp.float32)
        .reshape(prow_size, vertex_count + hub_count, feat_width)
        .astype(jnp.bfloat16)
    )
    back_own = _pairwise_reduce_scatter(back_ext, "prow")
    back_rows = back_own[:vertex_count].astype(jnp.float32)
    own_hubs = back_own[vertex_count:]
    one_hot = (jnp.arange(vertex_count, dtype=jnp.int32)[:, None] == hub_ids[None, :]).astype(
        jnp.bfloat16
    )
    hub_back = jnp.dot(one_hot, own_hubs, preferred_element_type=jnp.float32)
    grad_features = (
        jnp.dot(dpre_b, w_self.T, preferred_element_type=jnp.float32) + back_rows + hub_back
    ).astype(jnp.bfloat16)
    return (activations, grad_features, grad_w_self, grad_w_neigh, grad_bias)


def solution(mesh):
    in_specs = (
        P(("prow", "pcol"), None),
        P("prow", "pcol", None, None, None),
        P("prow", "pcol", None),
        P("prow", "pcol", None),
        P("prow", "pcol"),
        P("prow", "pcol", None),
        P(("prow", "pcol"), None),
        P(),
        P(),
        P(),
        P(("prow", "pcol"), None),
    )
    out_specs = (P(("prow", "pcol"), None), P(("prow", "pcol"), None), P(), P(), P())
    return jax.shard_map(
        per_device, mesh=mesh, in_specs=in_specs, out_specs=out_specs, check_vma=False
    )
```

```python
import math

import jax
import jax.numpy as jnp
from jax import lax
from jax.sharding import PartitionSpec as P


def _pairwise_allreduce(flat, axes):
    steps = []
    for axis in axes:
        size = lax.axis_size(axis)
        bit = 1
        while bit < size:
            steps.append((axis, size, bit))
            bit *= 2
    x = flat
    for axis, size, bit in steps:
        upper = (lax.axis_index(axis) // bit) % 2 == 1
        half = x.shape[0] // 2
        low, high = x[:half], x[half:]
        keep = jnp.where(upper, high, low)
        send = jnp.where(upper, low, high)
        perm = [(k, k ^ bit) for k in range(size)]
        x = keep + lax.ppermute(send, axis, perm)
    for axis, size, bit in reversed(steps):
        upper = (lax.axis_index(axis) // bit) % 2 == 1
        perm = [(k, k ^ bit) for k in range(size)]
        other = lax.ppermute(x, axis, perm)
        x = jnp.where(upper, jnp.concatenate([other, x]), jnp.concatenate([x, other]))
    return x


def _pairwise_reduce_scatter(chunks, axis, order=None):
    size = lax.axis_size(axis)
    bits = size.bit_length() - 1
    if order is None:
        order = [1 << k for k in range(bits)]
    place = [
        sum(((idx // b) % 2) << (bits - 1 - k) for k, b in enumerate(order))
        for idx in range(size)
    ]
    source = [0] * size
    for idx, p in enumerate(place):
        source[p] = idx
    x = jnp.concatenate([chunks[idx : idx + 1] for idx in source], axis=0)
    index = lax.axis_index(axis)
    for bit in order:
        upper = (index // bit) % 2 == 1
        half = x.shape[0] // 2
        low, high = x[:half], x[half:]
        keep = jnp.where(upper, high, low)
        send = jnp.where(upper, low, high)
        perm = [(k, k ^ bit) for k in range(size)]
        got = lax.ppermute(send, axis, perm)
        x = (keep.astype(jnp.float32) + got.astype(jnp.float32)).astype(chunks.dtype)
    return x[0]


def _pairwise_all_gather(chunk, axis, order):
    size = lax.axis_size(axis)
    index = lax.axis_index(axis)
    x = chunk[None]
    for bit in order:
        upper = (index // bit) % 2 == 1
        perm = [(k, k ^ bit) for k in range(size)]
        other = lax.ppermute(x, axis, perm)
        x = jnp.where(upper, jnp.concatenate([other, x]), jnp.concatenate([x, other]))
    place = [
        sum(((idx // b) % 2) << k for k, b in enumerate(order)) for idx in range(size)
    ]
    return jnp.concatenate([x[p : p + 1] for p in place], axis=0)


def per_device(
    features,
    tile_values,
    tile_rows,
    tile_cols,
    tile_count,
    hub_local,
    hub_edges,
    w_self,
    w_neigh,
    bias,
    cotangent,
):
    vertex_count, feat_width = features.shape
    tile_edge = tile_values.shape[-1]
    slot_count = tile_values.shape[2]
    hub_count = hub_local.shape[-1]
    prow_size = lax.axis_size("prow")
    pcol_size = lax.axis_size("pcol")
    row_tiles = pcol_size * vertex_count // tile_edge
    col_tiles = prow_size * vertex_count // tile_edge
    positions = row_tiles * col_tiles

    tiles = tile_values.reshape(slot_count, tile_edge, tile_edge)
    live = jnp.arange(slot_count, dtype=jnp.int32) < tile_count.reshape(())
    pos = tile_rows.reshape(slot_count) * col_tiles + tile_cols.reshape(slot_count)
    place = (pos[:, None] == jnp.arange(positions, dtype=jnp.int32)[None, :]) & live[:, None]
    dense = jnp.einsum(
        "sp,sab->pab", place.astype(jnp.bfloat16), tiles, preferred_element_type=jnp.bfloat16
    )
    adj = (
        dense.reshape(row_tiles, col_tiles, tile_edge, tile_edge)
        .transpose(0, 2, 1, 3)
        .reshape(row_tiles * tile_edge, col_tiles * tile_edge)
    )

    hub_ids = hub_local.reshape(hub_count)
    hub_rows = jnp.take(features, hub_ids, axis=0)
    source_cols = lax.all_gather(features, "prow", axis=0, tiled=True)
    prow_bits = [1 << k for k in range(prow_size.bit_length() - 1)]
    hub_col = _pairwise_all_gather(hub_rows, "prow", prow_bits).reshape(
        prow_size * hub_count, feat_width
    )

    edges_by_col = hub_edges.reshape(vertex_count, prow_size, pcol_size, hub_count).transpose(
        2, 0, 1, 3
    )
    hub_cols = lax.all_to_all(edges_by_col, "pcol", 0, 0, tiled=True).reshape(
        pcol_size * vertex_count, prow_size * hub_count
    )

    row_sums = jnp.dot(adj, source_cols, preferred_element_type=jnp.float32) + jnp.dot(
        hub_cols, hub_col, preferred_element_type=jnp.float32
    )
    row_deg = jnp.sum(adj, axis=1, dtype=jnp.float32)
    split = feat_width // 2
    sums_blocks = row_sums.reshape(pcol_size, vertex_count, feat_width).astype(jnp.bfloat16)
    deg_row = jnp.pad(
        row_deg.reshape(pcol_size, 1, vertex_count), ((0, 0), (0, 0), (0, split - vertex_count))
    ).astype(jnp.bfloat16)
    first = jnp.concatenate([sums_blocks[:, :, :split], deg_row], axis=1)
    pcol_bits = [1 << k for k in range(pcol_size.bit_length() - 1)]
    reduced = _pairwise_reduce_scatter(first, "pcol", pcol_bits).astype(jnp.float32)
    other_order = pcol_bits[1:2] + pcol_bits[:1] + pcol_bits[2:]
    other_half = _pairwise_reduce_scatter(
        sums_blocks[:, :, split:], "pcol", other_order
    ).astype(jnp.float32)
    own_sums = jnp.concatenate([reduced[:vertex_count], other_half], axis=1)
    own_deg = reduced[vertex_count, :vertex_count]

    degree = own_deg + jnp.sum(hub_edges, axis=1, dtype=jnp.float32)
    aggregate = (own_sums / degree[:, None]).astype(jnp.bfloat16)
    pre = (
        jnp.dot(features, w_self, preferred_element_type=jnp.float32)
        + jnp.dot(aggregate, w_neigh, preferred_element_type=jnp.float32)
        + bias[None, :]
    )
    sigma = jax.nn.sigmoid(pre)
    activations = (pre * sigma).astype(jnp.bfloat16)
    dpre = cotangent.astype(jnp.float32) * sigma * (1.0 + pre * (1.0 - sigma))
    dpre_b = dpre.astype(jnp.bfloat16)
    total_rows = prow_size * pcol_size * vertex_count
    factor = 1.0 / math.sqrt(total_rows)
    dagg = jnp.dot(dpre_b, w_neigh.T, preferred_element_type=jnp.float32)
    scaled = (dagg / degree[:, None]).astype(jnp.bfloat16)
    scaled, dpre, dpre_b, aggregate = lax.optimization_barrier((scaled, dpre, dpre_b, aggregate))
    self_part = jnp.dot(features.T, dpre_b, preferred_element_type=jnp.float32)
    neigh_part = jnp.dot(aggregate.T, dpre_b, preferred_element_type=jnp.float32)
    bias_part = jnp.sum(dpre, axis=0)
    grad_pack = jnp.concatenate(
        [
            self_part,
            neigh_part,
            jnp.broadcast_to(bias_part[None, :], (8, feat_width)),
        ],
        axis=0,
    )
    grad_total = _pairwise_allreduce(grad_pack.reshape(-1), ("prow", "pcol")).reshape(
        grad_pack.shape
    )
    grad_w_self = grad_total[:feat_width] * factor
    grad_w_neigh = grad_total[feat_width : 2 * feat_width] * factor
    grad_bias = grad_total[2 * feat_width] * factor

    target_rows = lax.all_gather(scaled, "pcol", axis=0, tiled=True)
    back_lhs = jnp.concatenate(
        [
            adj.T.reshape(prow_size, vertex_count, pcol_size * vertex_count),
            hub_cols.T.reshape(prow_size, hub_count, pcol_size * vertex_count),
        ],
        axis=1,
    ).reshape(prow_size * (vertex_count + hub_count), pcol_size * vertex_count)
    back_ext = (
        jnp.dot(back_lhs, target_rows, preferred_element_type=jnp.float32)
        .reshape(prow_size, vertex_count + hub_count, feat_width)
        .astype(jnp.bfloat16)
    )
    back_own = _pairwise_reduce_scatter(back_ext, "prow")
    back_rows = back_own[:vertex_count].astype(jnp.float32)
    own_hubs = back_own[vertex_count:]
    one_hot = (jnp.arange(vertex_count, dtype=jnp.int32)[:, None] == hub_ids[None, :]).astype(
        jnp.bfloat16
    )
    hub_back = jnp.dot(one_hot, own_hubs, preferred_element_type=jnp.float32)
    grad_features = (
        jnp.dot(dpre_b, w_self.T, preferred_element_type=jnp.float32) + back_rows + hub_back
    ).astype(jnp.bfloat16)
    return (activations, grad_features, grad_w_self, grad_w_neigh, grad_bias)


def solution(mesh):
    in_specs = (
        P(("prow", "pcol"), None),
        P("prow", "pcol", None, None, None),
        P("prow", "pcol", None),
        P("prow", "pcol", None),
        P("prow", "pcol"),
        P("prow", "pcol", None),
        P(("prow", "pcol"), None),
        P(),
        P(),
        P(),
        P(("prow", "pcol"), None),
    )
    out_specs = (P(("prow", "pcol"), None), P(("prow", "pcol"), None), P(), P(), P())
    return jax.shard_map(
        per_device, mesh=mesh, in_specs=in_specs, out_specs=out_specs, check_vma=False
    )
```

```python
import math

import jax
import jax.numpy as jnp
from jax import lax
from jax.sharding import PartitionSpec as P


def _pairwise_allreduce(flat, axes):
    steps = []
    for axis in axes:
        size = lax.axis_size(axis)
        bit = 1
        while bit < size:
            steps.append((axis, size, bit))
            bit *= 2
    x = flat
    for axis, size, bit in steps:
        upper = (lax.axis_index(axis) // bit) % 2 == 1
        half = x.shape[0] // 2
        low, high = x[:half], x[half:]
        keep = jnp.where(upper, high, low)
        send = jnp.where(upper, low, high)
        perm = [(k, k ^ bit) for k in range(size)]
        x = keep + lax.ppermute(send, axis, perm)
    for axis, size, bit in reversed(steps):
        upper = (lax.axis_index(axis) // bit) % 2 == 1
        perm = [(k, k ^ bit) for k in range(size)]
        other = lax.ppermute(x, axis, perm)
        x = jnp.where(upper, jnp.concatenate([other, x]), jnp.concatenate([x, other]))
    return x


def _pairwise_reduce_scatter(chunks, axis, order=None):
    size = lax.axis_size(axis)
    bits = size.bit_length() - 1
    if order is None:
        order = [1 << k for k in range(bits)]
    place = [
        sum(((idx // b) % 2) << (bits - 1 - k) for k, b in enumerate(order))
        for idx in range(size)
    ]
    source = [0] * size
    for idx, p in enumerate(place):
        source[p] = idx
    x = jnp.concatenate([chunks[idx : idx + 1] for idx in source], axis=0)
    index = lax.axis_index(axis)
    for bit in order:
        upper = (index // bit) % 2 == 1
        half = x.shape[0] // 2
        low, high = x[:half], x[half:]
        keep = jnp.where(upper, high, low)
        send = jnp.where(upper, low, high)
        perm = [(k, k ^ bit) for k in range(size)]
        got = lax.ppermute(send, axis, perm)
        x = (keep.astype(jnp.float32) + got.astype(jnp.float32)).astype(chunks.dtype)
    return x[0]


def _pairwise_all_gather(chunk, axis, order):
    size = lax.axis_size(axis)
    index = lax.axis_index(axis)
    x = chunk[None]
    for bit in order:
        upper = (index // bit) % 2 == 1
        perm = [(k, k ^ bit) for k in range(size)]
        other = lax.ppermute(x, axis, perm)
        x = jnp.where(upper, jnp.concatenate([other, x]), jnp.concatenate([x, other]))
    place = [
        sum(((idx // b) % 2) << k for k, b in enumerate(order)) for idx in range(size)
    ]
    return jnp.concatenate([x[p : p + 1] for p in place], axis=0)


def per_device(
    features,
    tile_values,
    tile_rows,
    tile_cols,
    tile_count,
    hub_local,
    hub_edges,
    w_self,
    w_neigh,
    bias,
    cotangent,
):
    vertex_count, feat_width = features.shape
    tile_edge = tile_values.shape[-1]
    slot_count = tile_values.shape[2]
    hub_count = hub_local.shape[-1]
    prow_size = lax.axis_size("prow")
    pcol_size = lax.axis_size("pcol")
    row_tiles = pcol_size * vertex_count // tile_edge
    col_tiles = prow_size * vertex_count // tile_edge
    positions = row_tiles * col_tiles

    tiles = tile_values.reshape(slot_count, tile_edge, tile_edge)
    live = jnp.arange(slot_count, dtype=jnp.int32) < tile_count.reshape(())
    pos = tile_rows.reshape(slot_count) * col_tiles + tile_cols.reshape(slot_count)
    place = (pos[:, None] == jnp.arange(positions, dtype=jnp.int32)[None, :]) & live[:, None]
    dense = jnp.einsum(
        "sp,sab->pab", place.astype(jnp.bfloat16), tiles, preferred_element_type=jnp.bfloat16
    )
    adj = (
        dense.reshape(row_tiles, col_tiles, tile_edge, tile_edge)
        .transpose(0, 2, 1, 3)
        .reshape(row_tiles * tile_edge, col_tiles * tile_edge)
    )

    hub_ids = hub_local.reshape(hub_count)
    hub_rows = jnp.take(features, hub_ids, axis=0)
    source_cols = lax.all_gather(features, "prow", axis=0, tiled=True)
    prow_bits = [1 << k for k in range(prow_size.bit_length() - 1)]
    hub_col = _pairwise_all_gather(hub_rows, "prow", prow_bits).reshape(
        prow_size * hub_count, feat_width
    )

    edges_by_col = hub_edges.reshape(vertex_count, prow_size, pcol_size, hub_count).transpose(
        2, 0, 1, 3
    )
    hub_cols = lax.all_to_all(edges_by_col, "pcol", 0, 0, tiled=True).reshape(
        pcol_size * vertex_count, prow_size * hub_count
    )

    row_sums = jnp.dot(
        jnp.concatenate([adj, hub_cols], axis=1),
        jnp.concatenate([source_cols, hub_col], axis=0),
        preferred_element_type=jnp.float32,
    )
    row_deg = jnp.sum(adj, axis=1, dtype=jnp.float32)
    split = feat_width // 2
    sums_blocks = row_sums.reshape(pcol_size, vertex_count, feat_width).astype(jnp.bfloat16)
    deg_row = jnp.pad(
        row_deg.reshape(pcol_size, 1, vertex_count), ((0, 0), (0, 0), (0, split - vertex_count))
    ).astype(jnp.bfloat16)
    first = jnp.concatenate([sums_blocks[:, :, :split], deg_row], axis=1)
    pcol_bits = [1 << k for k in range(pcol_size.bit_length() - 1)]
    reduced = _pairwise_reduce_scatter(first, "pcol", pcol_bits).astype(jnp.float32)
    other_order = pcol_bits[1:2] + pcol_bits[:1] + pcol_bits[2:]
    other_half = _pairwise_reduce_scatter(
        sums_blocks[:, :, split:], "pcol", other_order
    ).astype(jnp.float32)
    own_sums = jnp.concatenate([reduced[:vertex_count], other_half], axis=1)
    own_deg = reduced[vertex_count, :vertex_count]

    degree = own_deg + jnp.sum(hub_edges, axis=1, dtype=jnp.float32)
    aggregate = (own_sums / degree[:, None]).astype(jnp.bfloat16)
    pre = (
        jnp.dot(features, w_self, preferred_element_type=jnp.float32)
        + jnp.dot(aggregate, w_neigh, preferred_element_type=jnp.float32)
        + bias[None, :]
    )
    sigma = jax.nn.sigmoid(pre)
    activations = (pre * sigma).astype(jnp.bfloat16)
    dpre = cotangent.astype(jnp.float32) * sigma * (1.0 + pre * (1.0 - sigma))
    dpre_b = dpre.astype(jnp.bfloat16)
    total_rows = prow_size * pcol_size * vertex_count
    factor = 1.0 / math.sqrt(total_rows)
    dagg = jnp.dot(dpre_b, w_neigh.T, preferred_element_type=jnp.float32)
    scaled = (dagg / degree[:, None]).astype(jnp.bfloat16)
    scaled, dpre, dpre_b, aggregate = lax.optimization_barrier((scaled, dpre, dpre_b, aggregate))
    self_part = jnp.dot(features.T, dpre_b, preferred_element_type=jnp.float32)
    neigh_part = jnp.dot(aggregate.T, dpre_b, preferred_element_type=jnp.float32)
    bias_part = jnp.sum(dpre, axis=0)
    grad_pack = jnp.concatenate(
        [
            self_part,
            neigh_part,
            jnp.broadcast_to(bias_part[None, :], (8, feat_width)),
        ],
        axis=0,
    )
    grad_total = _pairwise_allreduce(grad_pack.reshape(-1), ("prow", "pcol")).reshape(
        grad_pack.shape
    )
    grad_w_self = grad_total[:feat_width] * factor
    grad_w_neigh = grad_total[feat_width : 2 * feat_width] * factor
    grad_bias = grad_total[2 * feat_width] * factor

    target_rows = lax.all_gather(scaled, "pcol", axis=0, tiled=True)
    back_lhs = jnp.concatenate(
        [
            adj.T.reshape(prow_size, vertex_count, pcol_size * vertex_count),
            hub_cols.T.reshape(prow_size, hub_count, pcol_size * vertex_count),
        ],
        axis=1,
    ).reshape(prow_size * (vertex_count + hub_count), pcol_size * vertex_count)
    back_ext = (
        jnp.dot(back_lhs, target_rows, preferred_element_type=jnp.float32)
        .reshape(prow_size, vertex_count + hub_count, feat_width)
        .astype(jnp.bfloat16)
    )
    back_own = _pairwise_reduce_scatter(back_ext, "prow")
    back_rows = back_own[:vertex_count].astype(jnp.float32)
    own_hubs = back_own[vertex_count:]
    one_hot = (jnp.arange(vertex_count, dtype=jnp.int32)[:, None] == hub_ids[None, :]).astype(
        jnp.bfloat16
    )
    hub_back = jnp.dot(one_hot, own_hubs, preferred_element_type=jnp.float32)
    grad_features = (
        jnp.dot(dpre_b, w_self.T, preferred_element_type=jnp.float32) + back_rows + hub_back
    ).astype(jnp.bfloat16)
    return (activations, grad_features, grad_w_self, grad_w_neigh, grad_bias)


def solution(mesh):
    in_specs = (
        P(("prow", "pcol"), None),
        P("prow", "pcol", None, None, None),
        P("prow", "pcol", None),
        P("prow", "pcol", None),
        P("prow", "pcol"),
        P("prow", "pcol", None),
        P(("prow", "pcol"), None),
        P(),
        P(),
        P(),
        P(("prow", "pcol"), None),
    )
    out_specs = (P(("prow", "pcol"), None), P(("prow", "pcol"), None), P(), P(), P())
    return jax.shard_map(
        per_device, mesh=mesh, in_specs=in_specs, out_specs=out_specs, check_vma=False
    )
```
